128 devices in a mesh: segment: 4 (over x), fsdp: 16 (over y, z_hi, core), rep: 2 (over z_lo).
Axes of the slice: x: 4, y: 4, z: 4 (z_hi: 2, z_lo: 2; z = z_hi * 2 + z_lo), core: 2. Of those that a mesh axis runs over, the one named last changes fastest.
Arguments:
- token_ids: int32 [128, 128], P('fsdp'), may hold values from 0 to 127
- seq_lengths: int32 [128], P('fsdp'), may hold values from 32 to 128, as said below
- quant_scores: int32 [128], P('fsdp'), may hold values from 0 to 64
- embed_table: bfloat16 [128, 4096], replicated, may hold values from -6 to 6
- prior_weight: bfloat16 [4, 4096, 4096], P('segment', None, 'rep'), may hold values from -0.09375 to 0.09375
- prior_gain: float32 [4, 4096], P('segment'), may hold values from 0.25 to 1.75
- final_gain: float32 [4096], replicated, may hold values from 0.25 to 1.75
- head_weight: bfloat16 [4096, 128], replicated, may hold values from -0.25 to 0.25
- agent_down: bfloat16 [4096, 256], P('fsdp'), may hold values from -0.09375 to 0.09375
- agent_up: bfloat16 [4096, 256], P('fsdp'), may hold values from -0.375 to 0.375
Outputs:
- down_gradient: float32 [4096, 256], P(('segment', 'fsdp', 'rep'))
- up_gradient: float32 [4096, 256], P(('segment', 'fsdp', 'rep'))
The draws below stay inside these ranges and needn't reach their ends.
Inputs may be any that keep to these rules, and one draw needn't show every extreme that they name: `seq_lengths`: every sequence keeps at least 32 tokens, and some sequence in every draw has all 128.
All inputs are finite; a program needn't handle non-finite values.
Results may differ from the reference program's by a relative error of at most 0.0081.
Values may be sent and summed in bfloat16 or wider, within the bound.
No kernel may reach another device: no remote copies, remote signals or barrier semaphores. Data moves between devices by JAX's collectives and lax.ppermute only.
A program may use at most 128 MiB of HBM per device.

```python
import jax
import jax.numpy as jnp
from jax import lax

D = 4096
V = 128
R = 256
L = 128
LEVELS = 64
SEQS = 128
N_SEGMENT = 4


def draw_seq_lengths(key, part):
    values = jax.random.randint(key, (SEQS,), L // 4, L + 1)
    return values.at[0].set(L).astype(jnp.int32)


def place_ends(result, own_key, smallest, high):
    spot = [jax.random.randint(jax.random.fold_in(own_key, axis), (), 0, length) for axis, length in enumerate(result.shape)]
    widest = result.shape.index(max(result.shape))
    beside = spot[:widest] + [(spot[widest] + 1) % result.shape[widest]] + spot[widest + 1:]
    return result.at[tuple(spot)].set(smallest).at[tuple(beside)].set(high)


def steps_of(key, extent, split, smallest, largest):
    factor_of = 1.0
    for dim, shards_of in split:
        draws = jax.random.uniform(jax.random.fold_in(jax.random.fold_in(key, 6), dim), (shards_of,), jnp.float32, smallest / len(split), largest / len(split))
        factor_of = factor_of * jnp.repeat(jnp.exp(draws), extent[dim] // shards_of).reshape((-1,) + (1,) * (len(extent) - 1 - dim))
    return factor_of


def centred(own_key, shape, spread, bound, cuts=(), kind=jnp.bfloat16):
    values = jax.random.normal(own_key, shape, jnp.float32) * spread
    if len(cuts) > 0:
        values = steps_of(own_key, shape, cuts, -0.22, 0.18) * values
    return jnp.clip(values, min=-bound, max=bound).astype(kind)


def setup_inputs(seed: int = 0) -> dict:
    keys = jax.random.split(jax.random.key(seed), 11)
    return {
        "token_ids": place_ends(jax.random.randint(keys[0], (SEQS, L), 0, V), jax.random.fold_in(keys[0], 1), 0, V - 1).astype(jnp.int32),
        "seq_lengths": draw_seq_lengths(jax.random.fold_in(keys[10], 71), 0),
        "quant_scores": place_ends(jax.random.randint(keys[2], (SEQS,), 0, LEVELS + 1), jax.random.fold_in(keys[2], 1), 0, LEVELS).astype(jnp.int32),
        "embed_table": centred(keys[3], (V, D), 1.0, 6.0),
        "prior_weight": centred(keys[4], (N_SEGMENT, D, D), D ** -0.5, 0.09375, ((0, 4), (2, 2))),
        "prior_gain": jnp.clip(1.0 + 0.15 * jax.random.normal(keys[5], (N_SEGMENT, D), jnp.float32), 0.25, 1.75),
        "final_gain": jnp.clip(1.0 + 0.15 * jax.random.normal(keys[6], (D,), jnp.float32), 0.25, 1.75),
        "head_weight": centred(keys[7], (D, V), (D // 9) ** -0.5, 0.25),
        "agent_down": centred(keys[8], (D, R), D ** -0.5, 0.09375, ((0, 16),)),
        "agent_up": centred(keys[9], (D, R), R ** -0.5, 0.375, ((0, 16),)),
    }


epsilon = 1e-05
sigma_weight = 2.0

def rms_scale(values):
    squares = lax.optimization_barrier(jnp.mean(values * values, axis=-1, keepdims=True))
    return lax.rsqrt(squares + epsilon)

def picked_logprob(logprob, targets):
    vocab_size = logprob.shape[-1]
    column = jnp.arange(vocab_size, dtype=jnp.int32)
    return lax.optimization_barrier(jnp.sum(jnp.where(column[None, :] == targets[:, None], logprob, 0.0), axis=-1))

def reference(token_ids, seq_lengths, quant_scores, embed_table, prior_weight, prior_gain, final_gain, head_weight, agent_down, agent_up):
    seq_total, seq_len = token_ids.shape
    vocab_size = embed_table.shape[0]
    flat_ids = token_ids.reshape(-1)
    next_ids = jnp.concatenate([token_ids[:, 1:], token_ids[:, :1]], axis=1).reshape(-1)
    positions = jnp.arange(seq_len, dtype=jnp.int32)
    live_mask = (positions[None, :] < seq_lengths[:, None] - 1).astype(jnp.float32)
    counts = (seq_lengths - 1).astype(jnp.float32)
    start_rows = jnp.take(embed_table, flat_ids, axis=0)
    rows_now = start_rows
    for segment_pos in range(N_SEGMENT):
        wide_rows = rows_now.astype(jnp.float32)
        normed = (wide_rows * rms_scale(wide_rows) * prior_gain[segment_pos]).astype(jnp.bfloat16)
        update = jnp.dot(normed, prior_weight[segment_pos], preferred_element_type=jnp.float32)
        rows_now = (wide_rows + update).astype(jnp.bfloat16)
    final_wide = rows_now.astype(jnp.float32)
    prior_final = (final_wide * rms_scale(final_wide) * final_gain).astype(jnp.bfloat16)
    prior_logp = jax.nn.log_softmax(jnp.dot(prior_final, head_weight, preferred_element_type=jnp.float32), axis=-1)
    prior_ll = lax.optimization_barrier(jnp.sum(picked_logprob(prior_logp, next_ids).reshape(seq_total, seq_len) * live_mask, axis=1)) / counts
    start_wide = start_rows.astype(jnp.float32)
    unit_rows = (start_wide * rms_scale(start_wide)).astype(jnp.bfloat16)
    latent = jnp.dot(unit_rows, agent_down, preferred_element_type=jnp.float32).astype(jnp.bfloat16)
    hidden = start_wide + jnp.dot(latent, agent_up.T, preferred_element_type=jnp.float32)
    inverse = rms_scale(hidden)
    agent_final = (hidden * inverse * final_gain).astype(jnp.bfloat16)
    agent_logp = jax.nn.log_softmax(jnp.dot(agent_final, head_weight, preferred_element_type=jnp.float32), axis=-1)
    agent_ll = lax.optimization_barrier(jnp.sum(picked_logprob(agent_logp, next_ids).reshape(seq_total, seq_len) * live_mask, axis=1)) / counts
    margin = prior_ll + sigma_weight * quant_scores.astype(jnp.float32) / LEVELS - agent_ll
    row_factor = ((2.0 * margin / counts)[:, None] * live_mask).reshape(-1)
    column = jnp.arange(vocab_size, dtype=jnp.int32)
    onehot_next = (next_ids[:, None] == column[None, :]).astype(jnp.float32)
    logit_grad = (row_factor[:, None] * (jnp.exp(agent_logp) - onehot_next)).astype(jnp.bfloat16)
    scaled_grad = jnp.dot(logit_grad, head_weight.T, preferred_element_type=jnp.float32) * final_gain
    hidden_grad = (inverse * scaled_grad - hidden * inverse * inverse * inverse * lax.optimization_barrier(jnp.mean(hidden * scaled_grad, axis=-1, keepdims=True))).astype(jnp.bfloat16)
    up_gradient = jnp.dot(hidden_grad.T, latent, preferred_element_type=jnp.float32)
    latent_grad = jnp.dot(hidden_grad, agent_up, preferred_element_type=jnp.float32).astype(jnp.bfloat16)
    down_gradient = jnp.dot(unit_rows.T, latent_grad, preferred_element_type=jnp.float32)
    return (down_gradient, up_gradient)
```

```python
import jax
import jax.numpy as jnp
from jax import lax
from jax.sharding import PartitionSpec as P

LEVELS = 64


epsilon = 1e-05
sigma_weight = 2.0


def rms_scale(values):
    squares = jnp.mean(values * values, axis=-1, keepdims=True)
    return lax.rsqrt(squares + epsilon)


def lookup_rows(row_ids, embed_table):
    vocab_size = embed_table.shape[0]
    column = jnp.arange(vocab_size, dtype=jnp.int32)
    onehot = (row_ids[:, None] == column[None, :]).astype(jnp.bfloat16)
    return jnp.dot(onehot, embed_table, preferred_element_type=jnp.float32).astype(jnp.bfloat16)


def picked_logprob(logprob, targets):
    vocab_size = logprob.shape[-1]
    column = jnp.arange(vocab_size, dtype=jnp.int32)
    return jnp.sum(jnp.where(column[None, :] == targets[:, None], logprob, 0.0), axis=-1)


def shifted(x, axis, size, by):
    return lax.ppermute(x, axis, [(i, (i + by) % size) for i in range(size)])


def fsdp_moved(x, mapping):
    return lax.ppermute(x, "fsdp", [(f, mapping(f)) for f in range(16)])


def ring_scatter(blocks, me, size, move):
    half = blocks.shape[-1] // 2
    ahead = blocks[..., :half]
    behind = blocks[..., half:]
    cur_a = lax.dynamic_index_in_dim(ahead, (me - 1) % size, 0, keepdims=False)
    cur_b = lax.dynamic_index_in_dim(behind, (me + 1) % size, 0, keepdims=False)
    for step in range(size - 1):
        got_a = move(cur_a, 1)
        got_b = move(cur_b, -1)
        cur_a = got_a + lax.dynamic_index_in_dim(ahead, (me - step - 2) % size, 0, keepdims=False)
        cur_b = got_b + lax.dynamic_index_in_dim(behind, (me + step + 2) % size, 0, keepdims=False)
    return jnp.concatenate([cur_a, cur_b], axis=-1)


def pair_scatter(blocks, axis_pos, me, move):
    keep = lax.dynamic_index_in_dim(blocks, me, axis_pos, keepdims=False)
    send = lax.dynamic_index_in_dim(blocks, 1 - me, axis_pos, keepdims=False)
    return keep + move(send)


def gradient_scatter(joined):
    rows, cols = joined.shape
    seg = lax.axis_index("segment")
    f = lax.axis_index("fsdp")
    rep = lax.axis_index("rep")
    y_pos = f // 4
    zh_pos = (f // 2) % 2
    core_pos = f % 2
    blocks = joined.reshape(4, 4, 2, 2, 2, rows // 128, cols)
    blocks = pair_scatter(blocks, 3, core_pos, lambda v: fsdp_moved(v, lambda g: g ^ 1))
    blocks = ring_scatter(blocks, seg, 4, lambda v, by: shifted(v, "segment", 4, by))
    blocks = ring_scatter(
        blocks, y_pos, 4, lambda v, by: fsdp_moved(v, lambda g: ((g // 4 + by) % 4) * 4 + g % 4)
    )
    blocks = pair_scatter(blocks, 1, rep, lambda v: shifted(v, "rep", 2, 1))
    blocks = pair_scatter(blocks, 0, zh_pos, lambda v: fsdp_moved(v, lambda g: g ^ 2))
    return blocks


def on_device(
    token_ids,
    seq_lengths,
    quant_scores,
    embed_table,
    prior_weight,
    prior_gain,
    final_gain,
    head_weight,
    agent_down,
    agent_up,
):
    segments = lax.axis_size("segment")
    replicas = lax.axis_size("rep")
    segment_pos = lax.axis_index("segment")
    rep_pos = lax.axis_index("rep")
    group_seqs, seq_len = token_ids.shape
    model_width = embed_table.shape[1]
    vocab_size = embed_table.shape[0]
    half_width = prior_weight.shape[2]
    per_device = group_seqs // (segments * replicas)
    micro_count = 8
    total_rows = group_seqs * seq_len
    block_rows = total_rows // micro_count
    tick_count = micro_count + 2 * (segments - 1)
    flat_ids = token_ids.reshape(-1)
    weight_local = prior_weight[0]
    gain_local = prior_gain[0]
    is_first = segment_pos == 0
    is_last = segment_pos == segments - 1
    own_first = rep_pos == 0

    down_full, up_full = (
        lax.all_gather(agent_down, "fsdp", axis=0, tiled=True),
        lax.all_gather(agent_up, "fsdp", axis=0, tiled=True),
    )

    def apply_segment(current):
        wide_rows = current.astype(jnp.float32)
        normed = (wide_rows * rms_scale(wide_rows) * gain_local).astype(jnp.bfloat16)
        update = jnp.dot(normed, weight_local, preferred_element_type=jnp.float32)
        own_half = lax.dynamic_slice_in_dim(wide_rows, rep_pos * half_width, half_width, 1)
        return (own_half + update).astype(jnp.bfloat16)

    def skip_segment(current):
        return jnp.zeros((block_rows, half_width), jnp.bfloat16)

    def tick_whole(tick_pos, state):
        arrived, computed, stored = state
        partner = shifted(arrived, "rep", replicas, 1)
        passed = lax.ppermute(computed, "segment", [(i, i + 1) for i in range(segments - 1)])
        micro_pos = tick_pos - 2 * segment_pos
        active = (micro_pos >= 0) & (micro_pos < micro_count)
        slot_pos = jnp.clip(micro_pos, 0, micro_count - 1)
        embedded = lookup_rows(
            lax.dynamic_slice_in_dim(flat_ids, slot_pos * block_rows, block_rows, 0), embed_table
        )
        low = jnp.where(own_first, arrived, partner)
        high = jnp.where(own_first, partner, arrived)
        joined = jnp.concatenate([low, high], axis=1)
        current = jnp.where(is_first, embedded, joined)
        result = lax.cond(active, apply_segment, skip_segment, current)
        previous = lax.dynamic_slice_in_dim(stored, slot_pos * block_rows, block_rows, 0)
        chosen = jnp.where(active & is_last, result, previous)
        stored = lax.dynamic_update_slice_in_dim(stored, chosen, slot_pos * block_rows, 0)
        return (passed, result, stored)

    initial = (
        jnp.zeros((block_rows, half_width), jnp.bfloat16),
        jnp.zeros((block_rows, half_width), jnp.bfloat16),
        jnp.zeros((total_rows, half_width), jnp.bfloat16),
    )
    final_half = lax.fori_loop(0, tick_count, tick_whole, initial)[2]

    positions = jnp.arange(seq_len, dtype=jnp.int32)
    next_ids = jnp.concatenate([token_ids[:, 1:], token_ids[:, :1]], axis=1)
    live_mask = (positions[None, :] < seq_lengths[:, None] - 1).astype(jnp.float32)
    counts = (seq_lengths - 1).astype(jnp.float32)

    wide_half = final_half.astype(jnp.float32)
    own_squares = jnp.sum(wide_half * wide_half, axis=-1, keepdims=True)
    squares = own_squares + shifted(own_squares, "rep", replicas, 1)
    final_scale = lax.rsqrt(squares / model_width + epsilon)
    gain_half = lax.dynamic_slice_in_dim(final_gain, rep_pos * half_width, half_width, 0)
    head_half = lax.dynamic_slice_in_dim(head_weight, rep_pos * half_width, half_width, 0)
    prior_half = (wide_half * final_scale * gain_half).astype(jnp.bfloat16)
    own_logits = jnp.dot(prior_half, head_half, preferred_element_type=jnp.float32)
    prior_logits = own_logits + shifted(own_logits, "rep", replicas, 1)
    prior_logp = jax.nn.log_softmax(prior_logits, axis=-1)
    token_terms = picked_logprob(prior_logp, next_ids.reshape(-1)).reshape(group_seqs, seq_len)
    prior_group = jnp.sum(token_terms * live_mask, axis=1) / counts
    from_last = prior_group
    for by in range(1, segments):
        moved = shifted(prior_group, "segment", segments, by)
        from_last = jnp.where((segment_pos - by) % segments == segments - 1, moved, from_last)
    prior_group = from_last

    own_seq = (segment_pos * replicas + rep_pos) * per_device
    prior_mine = lax.dynamic_slice_in_dim(prior_group, own_seq, per_device, 0)
    mine_ids = lax.dynamic_slice_in_dim(token_ids, own_seq, per_device, 0).reshape(-1)
    mine_next = lax.dynamic_slice_in_dim(next_ids, own_seq, per_device, 0).reshape(-1)
    mine_live = lax.dynamic_slice_in_dim(live_mask, own_seq, per_device, 0)
    mine_counts = lax.dynamic_slice_in_dim(counts, own_seq, per_device, 0)
    mine_scores = lax.dynamic_slice_in_dim(quant_scores, own_seq, per_device, 0)
    start_wide = lookup_rows(mine_ids, embed_table).astype(jnp.float32)
    unit_rows = (start_wide * rms_scale(start_wide)).astype(jnp.bfloat16)
    latent = jnp.dot(unit_rows, down_full, preferred_element_type=jnp.float32).astype(jnp.bfloat16)
    hidden = start_wide + lax.dot_general(
        latent, up_full, (((1,), (1,)), ((), ())), preferred_element_type=jnp.float32
    )
    inverse = rms_scale(hidden)
    agent_final = (hidden * inverse * final_gain).astype(jnp.bfloat16)
    logprob = jax.nn.log_softmax(
        jnp.dot(agent_final, head_weight, preferred_element_type=jnp.float32), axis=-1
    )
    agent_ll = (
        jnp.sum(picked_logprob(logprob, mine_next).reshape(per_device, seq_len) * mine_live, axis=1)
        / mine_counts
    )
    margin = prior_mine + sigma_weight * mine_scores.astype(jnp.float32) / LEVELS - agent_ll
    row_factor = ((2.0 * margin / mine_counts)[:, None] * mine_live).reshape(-1)
    column = jnp.arange(vocab_size, dtype=jnp.int32)
    onehot_next = (mine_next[:, None] == column[None, :]).astype(jnp.float32)
    logit_grad = (row_factor[:, None] * (jnp.exp(logprob) - onehot_next)).astype(jnp.bfloat16)
    scaled_grad = (
        lax.dot_general(
            logit_grad, head_weight, (((1,), (1,)), ((), ())), preferred_element_type=jnp.float32
        )
        * final_gain
    )
    hidden_grad = (
        inverse * scaled_grad
        - hidden
        * inverse
        * inverse
        * inverse
        * jnp.mean(hidden * scaled_grad, axis=-1, keepdims=True)
    ).astype(jnp.bfloat16)
    up_grad = lax.dot_general(
        hidden_grad, latent, (((0,), (0,)), ((), ())), preferred_element_type=jnp.float32
    )
    latent_grad = jnp.dot(hidden_grad, up_full, preferred_element_type=jnp.float32).astype(
        jnp.bfloat16
    )
    down_grad = lax.dot_general(
        unit_rows, latent_grad, (((0,), (0,)), ((), ())), preferred_element_type=jnp.float32
    )
    rank = down_grad.shape[1]
    shares = gradient_scatter(jnp.concatenate([down_grad, up_grad], axis=1))
    return (shares[:, :rank], shares[:, rank:])


def solution(mesh):
    placed = (
        P("fsdp", None),
        P("fsdp"),
        P("fsdp"),
        P(),
        P("segment", None, "rep"),
        P("segment", None),
        P(),
        P(),
        P("fsdp", None),
        P("fsdp", None),
    )
    return jax.shard_map(
        on_device,
        mesh=mesh,
        in_specs=placed,
        out_specs=(P(("segment", "fsdp", "rep"), None), P(("segment", "fsdp", "rep"), None)),
        check_vma=False,
    )
```

```python
import jax
import jax.numpy as jnp
from jax import lax
from jax.sharding import PartitionSpec as P

LEVELS = 64


epsilon = 1e-05
sigma_weight = 2.0


def rms_scale(values):
    squares = jnp.mean(values * values, axis=-1, keepdims=True)
    return lax.rsqrt(squares + epsilon)


def lookup_rows(row_ids, embed_table):
    vocab_size = embed_table.shape[0]
    column = jnp.arange(vocab_size, dtype=jnp.int32)
    onehot = (row_ids[:, None] == column[None, :]).astype(jnp.bfloat16)
    return jnp.dot(onehot, embed_table, preferred_element_type=jnp.float32).astype(jnp.bfloat16)


def picked_logprob(logprob, targets):
    vocab_size = logprob.shape[-1]
    column = jnp.arange(vocab_size, dtype=jnp.int32)
    return jnp.sum(jnp.where(column[None, :] == targets[:, None], logprob, 0.0), axis=-1)


def shifted(x, axis, size, by):
    return lax.ppermute(x, axis, [(i, (i + by) % size) for i in range(size)])


def fsdp_moved(x, mapping):
    return lax.ppermute(x, "fsdp", [(f, mapping(f)) for f in range(16)])


def ring_scatter(blocks, me, size, move):
    half = blocks.shape[-1] // 2
    ahead = blocks[..., :half]
    behind = blocks[..., half:]
    cur_a = lax.dynamic_index_in_dim(ahead, (me - 1) % size, 0, keepdims=False)
    cur_b = lax.dynamic_index_in_dim(behind, (me + 1) % size, 0, keepdims=False)
    for step in range(size - 1):
        got_a = move(cur_a, 1)
        got_b = move(cur_b, -1)
        cur_a = got_a + lax.dynamic_index_in_dim(ahead, (me - step - 2) % size, 0, keepdims=False)
        cur_b = got_b + lax.dynamic_index_in_dim(behind, (me + step + 2) % size, 0, keepdims=False)
    return jnp.concatenate([cur_a, cur_b], axis=-1)


def pair_scatter(blocks, axis_pos, me, move):
    keep = lax.dynamic_index_in_dim(blocks, me, axis_pos, keepdims=False)
    send = lax.dynamic_index_in_dim(blocks, 1 - me, axis_pos, keepdims=False)
    return keep + move(send)


def gradient_scatter(first, second):
    rows, cols = first.shape
    seg = lax.axis_index("segment")
    f = lax.axis_index("fsdp")
    rep = lax.axis_index("rep")
    y_pos = f // 4
    zh_pos = (f // 2) % 2
    core_pos = f % 2
    along_x = lambda v, by: shifted(v, "segment", 4, by)
    along_y = lambda v, by: fsdp_moved(v, lambda g: ((g // 4 + by) % 4) * 4 + g % 4)
    along_core = lambda v: fsdp_moved(v, lambda g: g ^ 1)
    along_zh = lambda v: fsdp_moved(v, lambda g: g ^ 2)
    along_zl = lambda v: shifted(v, "rep", 2, 1)
    outs = []
    for grad, order in ((first, 0), (second, 1)):
        blocks = grad.reshape(4, 4, 2, 2, 2, rows // 128, cols)
        blocks = pair_scatter(blocks, 3, core_pos, along_core)
        if order == 0:
            blocks = ring_scatter(blocks, seg, 4, along_x)
            blocks = ring_scatter(blocks, y_pos, 4, along_y)
        else:
            blocks = jnp.swapaxes(blocks, 0, 1)
            blocks = ring_scatter(blocks, y_pos, 4, along_y)
            blocks = ring_scatter(blocks, seg, 4, along_x)
        outs.append(blocks)
    outs = [pair_scatter(b, 1, rep, along_zl) for b in outs]
    outs = [pair_scatter(b, 0, zh_pos, along_zh) for b in outs]
    return outs


def on_device(
    token_ids,
    seq_lengths,
    quant_scores,
    embed_table,
    prior_weight,
    prior_gain,
    final_gain,
    head_weight,
    agent_down,
    agent_up,
):
    segments = lax.axis_size("segment")
    replicas = lax.axis_size("rep")
    segment_pos = lax.axis_index("segment")
    rep_pos = lax.axis_index("rep")
    group_seqs, seq_len = token_ids.shape
    model_width = embed_table.shape[1]
    vocab_size = embed_table.shape[0]
    half_width = prior_weight.shape[2]
    per_device = group_seqs // (segments * replicas)
    micro_count = 8
    total_rows = group_seqs * seq_len
    block_rows = total_rows // micro_count
    tick_count = micro_count + 2 * (segments - 1)
    flat_ids = token_ids.reshape(-1)
    weight_local = prior_weight[0]
    gain_local = prior_gain[0]
    is_first = segment_pos == 0
    is_last = segment_pos == segments - 1
    own_first = rep_pos == 0

    down_full, up_full = (
        lax.all_gather(agent_down, "fsdp", axis=0, tiled=True),
        lax.all_gather(agent_up, "fsdp", axis=0, tiled=True),
    )

    def apply_segment(current):
        wide_rows = current.astype(jnp.float32)
        normed = (wide_rows * rms_scale(wide_rows) * gain_local).astype(jnp.bfloat16)
        update = jnp.dot(normed, weight_local, preferred_element_type=jnp.float32)
        own_half = lax.dynamic_slice_in_dim(wide_rows, rep_pos * half_width, half_width, 1)
        return (own_half + update).astype(jnp.bfloat16)

    embedded_all = lookup_rows(flat_ids, embed_table)

    def tick_whole(tick_pos, state):
        arrived, computed, stored = state
        partner = shifted(arrived, "rep", replicas, 1)
        passed = lax.ppermute(computed, "segment", [(i, i + 1) for i in range(segments - 1)])
        micro_pos = tick_pos - 2 * segment_pos
        active = (micro_pos >= 0) & (micro_pos < micro_count)
        slot_pos = jnp.clip(micro_pos, 0, micro_count - 1)
        embedded = lax.dynamic_slice_in_dim(embedded_all, slot_pos * block_rows, block_rows, 0)
        low = jnp.where(own_first, arrived, partner)
        high = jnp.where(own_first, partner, arrived)
        joined = jnp.concatenate([low, high], axis=1)
        current = jnp.where(is_first, embedded, joined)
        result = apply_segment(current)
        previous = lax.dynamic_slice_in_dim(stored, slot_pos * block_rows, block_rows, 0)
        chosen = jnp.where(active & is_last, result, previous)
        stored = lax.dynamic_update_slice_in_dim(stored, chosen, slot_pos * block_rows, 0)
        return (passed, result, stored)

    initial = (
        jnp.zeros((block_rows, half_width), jnp.bfloat16),
        jnp.zeros((block_rows, half_width), jnp.bfloat16),
        jnp.zeros((total_rows, half_width), jnp.bfloat16),
    )
    final_half = lax.fori_loop(0, tick_count, tick_whole, initial)[2]

    positions = jnp.arange(seq_len, dtype=jnp.int32)
    next_ids = jnp.concatenate([token_ids[:, 1:], token_ids[:, :1]], axis=1)
    live_mask = (positions[None, :] < seq_lengths[:, None] - 1).astype(jnp.float32)
    counts = (seq_lengths - 1).astype(jnp.float32)

    wide_half = final_half.astype(jnp.float32)
    own_squares = jnp.sum(wide_half * wide_half, axis=-1, keepdims=True)
    squares = own_squares + shifted(own_squares, "rep", replicas, 1)
    final_scale = lax.rsqrt(squares / model_width + epsilon)
    gain_half = lax.dynamic_slice_in_dim(final_gain, rep_pos * half_width, half_width, 0)
    head_half = lax.dynamic_slice_in_dim(head_weight, rep_pos * half_width, half_width, 0)
    prior_half = (wide_half * final_scale * gain_half).astype(jnp.bfloat16)
    own_logits = jnp.dot(prior_half, head_half, preferred_element_type=jnp.float32)
    prior_logits = own_logits + shifted(own_logits, "rep", replicas, 1)
    prior_logp = jax.nn.log_softmax(prior_logits, axis=-1)
    token_terms = picked_logprob(prior_logp, next_ids.reshape(-1)).reshape(group_seqs, seq_len)
    prior_group = jnp.sum(token_terms * live_mask, axis=1) / counts
    from_last = prior_group
    for by in range(1, segments):
        moved = shifted(prior_group, "segment", segments, by)
        from_last = jnp.where((segment_pos - by) % segments == segments - 1, moved, from_last)
    prior_group = from_last

    own_seq = (segment_pos * replicas + rep_pos) * per_device
    prior_mine = lax.dynamic_slice_in_dim(prior_group, own_seq, per_device, 0)
    mine_ids = lax.dynamic_slice_in_dim(token_ids, own_seq, per_device, 0).reshape(-1)
    mine_next = lax.dynamic_slice_in_dim(next_ids, own_seq, per_device, 0).reshape(-1)
    mine_live = lax.dynamic_slice_in_dim(live_mask, own_seq, per_device, 0)
    mine_counts = lax.dynamic_slice_in_dim(counts, own_seq, per_device, 0)
    mine_scores = lax.dynamic_slice_in_dim(quant_scores, own_seq, per_device, 0)
    start_wide = lookup_rows(mine_ids, embed_table).astype(jnp.float32)
    unit_rows = (start_wide * rms_scale(start_wide)).astype(jnp.bfloat16)
    latent = jnp.dot(unit_rows, down_full, preferred_element_type=jnp.float32).astype(jnp.bfloat16)
    hidden = start_wide + lax.dot_general(
        latent, up_full, (((1,), (1,)), ((), ())), preferred_element_type=jnp.float32
    )
    inverse = rms_scale(hidden)
    agent_final = (hidden * inverse * final_gain).astype(jnp.bfloat16)
    logprob = jax.nn.log_softmax(
        jnp.dot(agent_final, head_weight, preferred_element_type=jnp.float32), axis=-1
    )
    agent_ll = (
        jnp.sum(picked_logprob(logprob, mine_next).reshape(per_device, seq_len) * mine_live, axis=1)
        / mine_counts
    )
    margin = prior_mine + sigma_weight * mine_scores.astype(jnp.float32) / LEVELS - agent_ll
    row_factor = ((2.0 * margin / mine_counts)[:, None] * mine_live).reshape(-1)
    column = jnp.arange(vocab_size, dtype=jnp.int32)
    onehot_next = (mine_next[:, None] == column[None, :]).astype(jnp.float32)
    logit_grad = (row_factor[:, None] * (jnp.exp(logprob) - onehot_next)).astype(jnp.bfloat16)
    scaled_grad = (
        lax.dot_general(
            logit_grad, head_weight, (((1,), (1,)), ((), ())), preferred_element_type=jnp.float32
        )
        * final_gain
    )
    hidden_grad = (
        inverse * scaled_grad
        - hidden
        * inverse
        * inverse
        * inverse
        * jnp.mean(hidden * scaled_grad, axis=-1, keepdims=True)
    ).astype(jnp.bfloat16)
    up_grad = lax.dot_general(
        hidden_grad, latent, (((0,), (0,)), ((), ())), preferred_element_type=jnp.float32
    )
    latent_grad = jnp.dot(hidden_grad, up_full, preferred_element_type=jnp.float32).astype(
        jnp.bfloat16
    )
    down_grad = lax.dot_general(
        unit_rows, latent_grad, (((0,), (0,)), ((), ())), preferred_element_type=jnp.float32
    )
    down_share, up_share = gradient_scatter(down_grad, up_grad)
    return (down_share, up_share)


def solution(mesh):
    placed = (
        P("fsdp", None),
        P("fsdp"),
        P("fsdp"),
        P(),
        P("segment", None, "rep"),
        P("segment", None),
        P(),
        P(),
        P("fsdp", None),
        P("fsdp", None),
    )
    return jax.shard_map(
        on_device,
        mesh=mesh,
        in_specs=placed,
        out_specs=(P(("segment", "fsdp", "rep"), None), P(("segment", "fsdp", "rep"), None)),
        check_vma=False,
    )
```

```python
import jax
import jax.numpy as jnp
from jax import lax
from jax.sharding import PartitionSpec as P

LEVELS = 64


epsilon = 1e-05
sigma_weight = 2.0


def rms_scale(values):
    squares = jnp.mean(values * values, axis=-1, keepdims=True)
    return lax.rsqrt(squares + epsilon)


def lookup_rows(row_ids, embed_table):
    vocab_size = embed_table.shape[0]
    column = jnp.arange(vocab_size, dtype=jnp.int32)
    onehot = (row_ids[:, None] == column[None, :]).astype(jnp.bfloat16)
    return jnp.dot(onehot, embed_table, preferred_element_type=jnp.float32).astype(jnp.bfloat16)


def picked_logprob(logprob, targets):
    vocab_size = logprob.shape[-1]
    column = jnp.arange(vocab_size, dtype=jnp.int32)
    return jnp.sum(jnp.where(column[None, :] == targets[:, None], logprob, 0.0), axis=-1)


def shifted(x, axis, size, by):
    return lax.ppermute(x, axis, [(i, (i + by) % size) for i in range(size)])


def fsdp_moved(x, mapping):
    return lax.ppermute(x, "fsdp", [(f, mapping(f)) for f in range(16)])


def ring_scatter(blocks, me, size, move):
    half = blocks.shape[-1] // 2
    ahead = blocks[..., :half]
    behind = blocks[..., half:]
    cur_a = lax.dynamic_index_in_dim(ahead, (me - 1) % size, 0, keepdims=False)
    cur_b = lax.dynamic_index_in_dim(behind, (me + 1) % size, 0, keepdims=False)
    for step in range(size - 1):
        got_a = move(cur_a, 1)
        got_b = move(cur_b, -1)
        cur_a = got_a + lax.dynamic_index_in_dim(ahead, (me - step - 2) % size, 0, keepdims=False)
        cur_b = got_b + lax.dynamic_index_in_dim(behind, (me + step + 2) % size, 0, keepdims=False)
    return jnp.concatenate([cur_a, cur_b], axis=-1)


def pair_scatter(blocks, axis_pos, me, move):
    keep = lax.dynamic_index_in_dim(blocks, me, axis_pos, keepdims=False)
    send = lax.dynamic_index_in_dim(blocks, 1 - me, axis_pos, keepdims=False)
    return keep + move(send)


def gradient_scatter(first, second):
    rows, cols = first.shape
    seg = lax.axis_index("segment")
    f = lax.axis_index("fsdp")
    rep = lax.axis_index("rep")
    y_pos = f // 4
    zh_pos = (f // 2) % 2
    core_pos = f % 2
    along_x = lambda v, by: shifted(v, "segment", 4, by)
    along_y = lambda v, by: fsdp_moved(v, lambda g: ((g // 4 + by) % 4) * 4 + g % 4)
    along_core = lambda v: fsdp_moved(v, lambda g: g ^ 1)
    along_zh = lambda v: fsdp_moved(v, lambda g: g ^ 2)
    along_zl = lambda v: shifted(v, "rep", 2, 1)
    outs = []
    for grad, order in ((first, 0), (second, 1)):
        blocks = grad.reshape(4, 4, 2, 2, 2, rows // 128, cols)
        blocks = pair_scatter(blocks, 3, core_pos, along_core)
        if order == 0:
            blocks = ring_scatter(blocks, seg, 4, along_x)
            blocks = ring_scatter(blocks, y_pos, 4, along_y)
        else:
            blocks = jnp.swapaxes(blocks, 0, 1)
            blocks = ring_scatter(blocks, y_pos, 4, along_y)
            blocks = ring_scatter(blocks, seg, 4, along_x)
        outs.append(blocks)
    outs = [pair_scatter(b, 1, rep, along_zl) for b in outs]
    outs = [pair_scatter(b, 0, zh_pos, along_zh) for b in outs]
    return outs


def on_device(
    token_ids,
    seq_lengths,
    quant_scores,
    embed_table,
    prior_weight,
    prior_gain,
    final_gain,
    head_weight,
    agent_down,
    agent_up,
):
    segments = lax.axis_size("segment")
    replicas = lax.axis_size("rep")
    segment_pos = lax.axis_index("segment")
    rep_pos = lax.axis_index("rep")
    group_seqs, seq_len = token_ids.shape
    model_width = embed_table.shape[1]
    vocab_size = embed_table.shape[0]
    half_width = prior_weight.shape[2]
    per_device = group_seqs // (segments * replicas)
    micro_count = 4
    total_rows = group_seqs * seq_len
    block_rows = total_rows // micro_count
    tick_count = micro_count + 2 * (segments - 1)
    flat_ids = token_ids.reshape(-1)
    weight_local = prior_weight[0]
    gain_local = prior_gain[0]
    is_first = segment_pos == 0
    is_last = segment_pos == segments - 1
    own_first = rep_pos == 0

    down_full, up_full = (
        lax.all_gather(agent_down, "fsdp", axis=0, tiled=True),
        lax.all_gather(agent_up, "fsdp", axis=0, tiled=True),
    )

    def apply_segment(current):
        wide_rows = current.astype(jnp.float32)
        normed = (wide_rows * rms_scale(wide_rows) * gain_local).astype(jnp.bfloat16)
        update = jnp.dot(normed, weight_local, preferred_element_type=jnp.float32)
        own_half = lax.dynamic_slice_in_dim(wide_rows, rep_pos * half_width, half_width, 1)
        return (own_half + update).astype(jnp.bfloat16)

    embedded_all = lookup_rows(flat_ids, embed_table)

    def tick_whole(tick_pos, state):
        arrived, computed, stored = state
        partner = shifted(arrived, "rep", replicas, 1)
        passed = lax.ppermute(computed, "segment", [(i, i + 1) for i in range(segments - 1)])
        micro_pos = tick_pos - 2 * segment_pos
        active = (micro_pos >= 0) & (micro_pos < micro_count)
        slot_pos = jnp.clip(micro_pos, 0, micro_count - 1)
        embedded = lax.dynamic_slice_in_dim(embedded_all, slot_pos * block_rows, block_rows, 0)
        low = jnp.where(own_first, arrived, partner)
        high = jnp.where(own_first, partner, arrived)
        joined = jnp.concatenate([low, high], axis=1)
        current = jnp.where(is_first, embedded, joined)
        result = apply_segment(current)
        previous = lax.dynamic_slice_in_dim(stored, slot_pos * block_rows, block_rows, 0)
        chosen = jnp.where(active & is_last, result, previous)
        stored = lax.dynamic_update_slice_in_dim(stored, chosen, slot_pos * block_rows, 0)
        return (passed, result, stored)

    initial = (
        jnp.zeros((block_rows, half_width), jnp.bfloat16),
        jnp.zeros((block_rows, half_width), jnp.bfloat16),
        jnp.zeros((total_rows, half_width), jnp.bfloat16),
    )
    final_half = lax.fori_loop(0, tick_count, tick_whole, initial)[2]

    positions = jnp.arange(seq_len, dtype=jnp.int32)
    next_ids = jnp.concatenate([token_ids[:, 1:], token_ids[:, :1]], axis=1)
    live_mask = (positions[None, :] < seq_lengths[:, None] - 1).astype(jnp.float32)
    counts = (seq_lengths - 1).astype(jnp.float32)

    wide_half = final_half.astype(jnp.float32)
    own_squares = jnp.sum(wide_half * wide_half, axis=-1, keepdims=True)
    squares = own_squares + shifted(own_squares, "rep", replicas, 1)
    final_scale = lax.rsqrt(squares / model_width + epsilon)
    gain_half = lax.dynamic_slice_in_dim(final_gain, rep_pos * half_width, half_width, 0)
    head_half = lax.dynamic_slice_in_dim(head_weight, rep_pos * half_width, half_width, 0)
    prior_half = (wide_half * final_scale * gain_half).astype(jnp.bfloat16)
    own_logits = jnp.dot(prior_half, head_half, preferred_element_type=jnp.float32)
    prior_logits = own_logits + shifted(own_logits, "rep", replicas, 1)
    prior_logp = jax.nn.log_softmax(prior_logits, axis=-1)
    token_terms = picked_logprob(prior_logp, next_ids.reshape(-1)).reshape(group_seqs, seq_len)
    prior_group = jnp.sum(token_terms * live_mask, axis=1) / counts
    from_last = prior_group
    for by in range(1, segments):
        moved = shifted(prior_group, "segment", segments, by)
        from_last = jnp.where((segment_pos - by) % segments == segments - 1, moved, from_last)
    prior_group = from_last

    own_seq = (segment_pos * replicas + rep_pos) * per_device
    prior_mine = lax.dynamic_slice_in_dim(prior_group, own_seq, per_device, 0)
    mine_ids = lax.dynamic_slice_in_dim(token_ids, own_seq, per_device, 0).reshape(-1)
    mine_next = lax.dynamic_slice_in_dim(next_ids, own_seq, per_device, 0).reshape(-1)
    mine_live = lax.dynamic_slice_in_dim(live_mask, own_seq, per_device, 0)
    mine_counts = lax.dynamic_slice_in_dim(counts, own_seq, per_device, 0)
    mine_scores = lax.dynamic_slice_in_dim(quant_scores, own_seq, per_device, 0)
    start_wide = lookup_rows(mine_ids, embed_table).astype(jnp.float32)
    unit_rows = (start_wide * rms_scale(start_wide)).astype(jnp.bfloat16)
    latent = jnp.dot(unit_rows, down_full, preferred_element_type=jnp.float32).astype(jnp.bfloat16)
    hidden = start_wide + lax.dot_general(
        latent, up_full, (((1,), (1,)), ((), ())), preferred_element_type=jnp.float32
    )
    inverse = rms_scale(hidden)
    agent_final = (hidden * inverse * final_gain).astype(jnp.bfloat16)
    logprob = jax.nn.log_softmax(
        jnp.dot(agent_final, head_weight, preferred_element_type=jnp.float32), axis=-1
    )
    agent_ll = (
        jnp.sum(picked_logprob(logprob, mine_next).reshape(per_device, seq_len) * mine_live, axis=1)
        / mine_counts
    )
    margin = prior_mine + sigma_weight * mine_scores.astype(jnp.float32) / LEVELS - agent_ll
    row_factor = ((2.0 * margin / mine_counts)[:, None] * mine_live).reshape(-1)
    column = jnp.arange(vocab_size, dtype=jnp.int32)
    onehot_next = (mine_next[:, None] == column[None, :]).astype(jnp.float32)
    logit_grad = (row_factor[:, None] * (jnp.exp(logprob) - onehot_next)).astype(jnp.bfloat16)
    scaled_grad = (
        lax.dot_general(
            logit_grad, head_weight, (((1,), (1,)), ((), ())), preferred_element_type=jnp.float32
        )
        * final_gain
    )
    hidden_grad = (
        inverse * scaled_grad
        - hidden
        * inverse
        * inverse
        * inverse
        * jnp.mean(hidden * scaled_grad, axis=-1, keepdims=True)
    ).astype(jnp.bfloat16)
    up_grad = lax.dot_general(
        hidden_grad, latent, (((0,), (0,)), ((), ())), preferred_element_type=jnp.float32
    )
    latent_grad = jnp.dot(hidden_grad, up_full, preferred_element_type=jnp.float32).astype(
        jnp.bfloat16
    )
    down_grad = lax.dot_general(
        unit_rows, latent_grad, (((0,), (0,)), ((), ())), preferred_element_type=jnp.float32
    )
    down_share, up_share = gradient_scatter(down_grad, up_grad)
    return (down_share, up_share)


def solution(mesh):
    placed = (
        P("fsdp", None),
        P("fsdp"),
        P("fsdp"),
        P(),
        P("segment", None, "rep"),
        P("segment", None),
        P(),
        P(),
        P("fsdp", None),
        P("fsdp", None),
    )
    return jax.shard_map(
        on_device,
        mesh=mesh,
        in_specs=placed,
        out_specs=(P(("segment", "fsdp", "rep"), None), P(("segment", "fsdp", "rep"), None)),
        check_vma=False,
    )
```

```python
import jax
import jax.numpy as jnp
from jax import lax
from jax.sharding import PartitionSpec as P

LEVELS = 64


epsilon = 1e-05
sigma_weight = 2.0


def rms_scale(values):
    squares = jnp.mean(values * values, axis=-1, keepdims=True)
    return lax.rsqrt(squares + epsilon)


def lookup_rows(row_ids, embed_table):
    vocab_size = embed_table.shape[0]
    column = jnp.arange(vocab_size, dtype=jnp.int32)
    onehot = (row_ids[:, None] == column[None, :]).astype(jnp.bfloat16)
    return jnp.dot(onehot, embed_table, preferred_element_type=jnp.float32).astype(jnp.bfloat16)


def picked_logprob(logprob, targets):
    vocab_size = logprob.shape[-1]
    column = jnp.arange(vocab_size, dtype=jnp.int32)
    return jnp.sum(jnp.where(column[None, :] == targets[:, None], logprob, 0.0), axis=-1)


def shifted(x, axis, size, by):
    return lax.ppermute(x, axis, [(i, (i + by) % size) for i in range(size)])


def fsdp_moved(x, mapping):
    return lax.ppermute(x, "fsdp", [(f, mapping(f)) for f in range(16)])


def ring_scatter(blocks, me, size, move):
    half = blocks.shape[-1] // 2
    ahead = blocks[..., :half]
    behind = blocks[..., half:]
    cur_a = lax.dynamic_index_in_dim(ahead, (me - 1) % size, 0, keepdims=False)
    cur_b = lax.dynamic_index_in_dim(behind, (me + 1) % size, 0, keepdims=False)
    for step in range(size - 1):
        got_a = move(cur_a, 1)
        got_b = move(cur_b, -1)
        cur_a = got_a + lax.dynamic_index_in_dim(ahead, (me - step - 2) % size, 0, keepdims=False)
        cur_b = got_b + lax.dynamic_index_in_dim(behind, (me + step + 2) % size, 0, keepdims=False)
    return jnp.concatenate([cur_a, cur_b], axis=-1)


def pair_scatter(blocks, axis_pos, me, move):
    keep = lax.dynamic_index_in_dim(blocks, me, axis_pos, keepdims=False)
    send = lax.dynamic_index_in_dim(blocks, 1 - me, axis_pos, keepdims=False)
    return keep + move(send)


def gradient_scatter(first, second):
    rows, cols = first.shape
    seg = lax.axis_index("segment")
    f = lax.axis_index("fsdp")
    rep = lax.axis_index("rep")
    y_pos = f // 4
    zh_pos = (f // 2) % 2
    core_pos = f % 2
    along_x = lambda v, by: shifted(v, "segment", 4, by)
    along_y = lambda v, by: fsdp_moved(v, lambda g: ((g // 4 + by) % 4) * 4 + g % 4)
    along_core = lambda v: fsdp_moved(v, lambda g: g ^ 1)
    along_zh = lambda v: fsdp_moved(v, lambda g: g ^ 2)
    along_zl = lambda v: shifted(v, "rep", 2, 1)
    both = jnp.stack([first, second]).reshape(2, 4, 4, 2, 2, 2, rows // 128, cols)
    both = pair_scatter(both, 4, core_pos, along_core)
    outs = []
    for order in (0, 1):
        blocks = both[order]
        if order == 0:
            blocks = ring_scatter(blocks, seg, 4, along_x)
            blocks = ring_scatter(blocks, y_pos, 4, along_y)
        else:
            blocks = jnp.swapaxes(blocks, 0, 1)
            blocks = ring_scatter(blocks, y_pos, 4, along_y)
            blocks = ring_scatter(blocks, seg, 4, along_x)
        outs.append(blocks)
    both = jnp.stack(outs)
    both = pair_scatter(both, 2, rep, along_zl)
    both = pair_scatter(both, 1, zh_pos, along_zh)
    outs = [both[0], both[1]]
    return outs


def on_device(
    token_ids,
    seq_lengths,
    quant_scores,
    embed_table,
    prior_weight,
    prior_gain,
    final_gain,
    head_weight,
    agent_down,
    agent_up,
):
    segments = lax.axis_size("segment")
    replicas = lax.axis_size("rep")
    segment_pos = lax.axis_index("segment")
    rep_pos = lax.axis_index("rep")
    group_seqs, seq_len = token_ids.shape
    model_width = embed_table.shape[1]
    vocab_size = embed_table.shape[0]
    half_width = prior_weight.shape[2]
    per_device = group_seqs // (segments * replicas)
    micro_count = 8
    total_rows = group_seqs * seq_len
    block_rows = total_rows // micro_count
    tick_count = micro_count + 2 * (segments - 1)
    flat_ids = token_ids.reshape(-1)
    weight_local = prior_weight[0]
    gain_local = prior_gain[0]
    is_first = segment_pos == 0
    is_last = segment_pos == segments - 1
    own_first = rep_pos == 0

    down_full, up_full = (
        lax.all_gather(agent_down, "fsdp", axis=0, tiled=True),
        lax.all_gather(agent_up, "fsdp", axis=0, tiled=True),
    )

    gain_own = lax.dynamic_slice_in_dim(gain_local, rep_pos * half_width, half_width, 0)
    gain_other = lax.dynamic_slice_in_dim(gain_local, (1 - rep_pos) * half_width, half_width, 0)
    weight_own = lax.dynamic_slice_in_dim(weight_local, rep_pos * half_width, half_width, 0)
    weight_other = lax.dynamic_slice_in_dim(weight_local, (1 - rep_pos) * half_width, half_width, 0)
    embedded_all = lookup_rows(flat_ids, embed_table)
    embedded_own = lax.dynamic_slice_in_dim(embedded_all, rep_pos * half_width, half_width, 1)

    def tick_whole(tick_pos, state):
        arrived, computed, stored = state
        micro_pos = tick_pos - 2 * segment_pos
        active = (micro_pos >= 0) & (micro_pos < micro_count)
        slot_pos = jnp.clip(micro_pos, 0, micro_count - 1)
        embedded = lax.dynamic_slice_in_dim(embedded_own, slot_pos * block_rows, block_rows, 0)
        own_rows = jnp.where(is_first, embedded, arrived)
        partner = shifted(own_rows, "rep", replicas, 1)
        passed = lax.ppermute(computed, "segment", [(i, i + 1) for i in range(segments - 1)])
        own_wide = own_rows.astype(jnp.float32)
        own_squares = jnp.sum(own_wide * own_wide, axis=-1, keepdims=True)
        squares = own_squares + shifted(own_squares, "rep", replicas, 1)
        scale = lax.rsqrt(squares / model_width + epsilon)
        normed_own = (own_wide * scale * gain_own).astype(jnp.bfloat16)
        normed_other = (partner.astype(jnp.float32) * scale * gain_other).astype(jnp.bfloat16)
        update = jnp.dot(normed_own, weight_own, preferred_element_type=jnp.float32) + jnp.dot(
            normed_other, weight_other, preferred_element_type=jnp.float32
        )
        result = (own_wide + update).astype(jnp.bfloat16)
        previous = lax.dynamic_slice_in_dim(stored, slot_pos * block_rows, block_rows, 0)
        chosen = jnp.where(active & is_last, result, previous)
        stored = lax.dynamic_update_slice_in_dim(stored, chosen, slot_pos * block_rows, 0)
        return (passed, result, stored)

    initial = (
        jnp.zeros((block_rows, half_width), jnp.bfloat16),
        jnp.zeros((block_rows, half_width), jnp.bfloat16),
        jnp.zeros((total_rows, half_width), jnp.bfloat16),
    )
    final_half = lax.fori_loop(0, tick_count, tick_whole, initial)[2]

    positions = jnp.arange(seq_len, dtype=jnp.int32)
    next_ids = jnp.concatenate([token_ids[:, 1:], token_ids[:, :1]], axis=1)
    live_mask = (positions[None, :] < seq_lengths[:, None] - 1).astype(jnp.float32)
    counts = (seq_lengths - 1).astype(jnp.float32)

    wide_half = final_half.astype(jnp.float32)
    own_squares = jnp.sum(wide_half * wide_half, axis=-1, keepdims=True)
    squares = own_squares + shifted(own_squares, "rep", replicas, 1)
    final_scale = lax.rsqrt(squares / model_width + epsilon)
    gain_half = lax.dynamic_slice_in_dim(final_gain, rep_pos * half_width, half_width, 0)
    head_half = lax.dynamic_slice_in_dim(head_weight, rep_pos * half_width, half_width, 0)
    prior_half = (wide_half * final_scale * gain_half).astype(jnp.bfloat16)
    own_logits = jnp.dot(prior_half, head_half, preferred_element_type=jnp.float32)
    prior_logits = own_logits + shifted(own_logits, "rep", replicas, 1)
    prior_logp = jax.nn.log_softmax(prior_logits, axis=-1)
    token_terms = picked_logprob(prior_logp, next_ids.reshape(-1)).reshape(group_seqs, seq_len)
    prior_group = jnp.sum(token_terms * live_mask, axis=1) / counts
    from_last = prior_group
    for by in range(1, segments):
        moved = shifted(prior_group, "segment", segments, by)
        from_last = jnp.where((segment_pos - by) % segments == segments - 1, moved, from_last)
    prior_group = from_last

    own_seq = (segment_pos * replicas + rep_pos) * per_device
    prior_mine = lax.dynamic_slice_in_dim(prior_group, own_seq, per_device, 0)
    mine_ids = lax.dynamic_slice_in_dim(token_ids, own_seq, per_device, 0).reshape(-1)
    mine_next = lax.dynamic_slice_in_dim(next_ids, own_seq, per_device, 0).reshape(-1)
    mine_live = lax.dynamic_slice_in_dim(live_mask, own_seq, per_device, 0)
    mine_counts = lax.dynamic_slice_in_dim(counts, own_seq, per_device, 0)
    mine_scores = lax.dynamic_slice_in_dim(quant_scores, own_seq, per_device, 0)
    start_wide = lookup_rows(mine_ids, embed_table).astype(jnp.float32)
    unit_rows = (start_wide * rms_scale(start_wide)).astype(jnp.bfloat16)
    latent = jnp.dot(unit_rows, down_full, preferred_element_type=jnp.float32).astype(jnp.bfloat16)
    hidden = start_wide + lax.dot_general(
        latent, up_full, (((1,), (1,)), ((), ())), preferred_element_type=jnp.float32
    )
    inverse = rms_scale(hidden)
    agent_final = (hidden * inverse * final_gain).astype(jnp.bfloat16)
    logprob = jax.nn.log_softmax(
        jnp.dot(agent_final, head_weight, preferred_element_type=jnp.float32), axis=-1
    )
    agent_ll = (
        jnp.sum(picked_logprob(logprob, mine_next).reshape(per_device, seq_len) * mine_live, axis=1)
        / mine_counts
    )
    margin = prior_mine + sigma_weight * mine_scores.astype(jnp.float32) / LEVELS - agent_ll
    row_factor = ((2.0 * margin / mine_counts)[:, None] * mine_live).reshape(-1)
    column = jnp.arange(vocab_size, dtype=jnp.int32)
    onehot_next = (mine_next[:, None] == column[None, :]).astype(jnp.float32)
    logit_grad = (row_factor[:, None] * (jnp.exp(logprob) - onehot_next)).astype(jnp.bfloat16)
    scaled_grad = (
        lax.dot_general(
            logit_grad, head_weight, (((1,), (1,)), ((), ())), preferred_element_type=jnp.float32
        )
        * final_gain
    )
    hidden_grad = (
        inverse * scaled_grad
        - hidden
        * inverse
        * inverse
        * inverse
        * jnp.mean(hidden * scaled_grad, axis=-1, keepdims=True)
    ).astype(jnp.bfloat16)
    up_grad = lax.dot_general(
        hidden_grad, latent, (((0,), (0,)), ((), ())), preferred_element_type=jnp.float32
    )
    latent_grad = jnp.dot(hidden_grad, up_full, preferred_element_type=jnp.float32).astype(
        jnp.bfloat16
    )
    down_grad = lax.dot_general(
        unit_rows, latent_grad, (((0,), (0,)), ((), ())), preferred_element_type=jnp.float32
    )
    down_share, up_share = gradient_scatter(down_grad, up_grad)
    return (down_share, up_share)


def solution(mesh):
    placed = (
        P("fsdp", None),
        P("fsdp"),
        P("fsdp"),
        P(),
        P("segment", None, "rep"),
        P("segment", None),
        P(),
        P(),
        P("fsdp", None),
        P("fsdp", None),
    )
    return jax.shard_map(
        on_device,
        mesh=mesh,
        in_specs=placed,
        out_specs=(P(("segment", "fsdp", "rep"), None), P(("segment", "fsdp", "rep"), None)),
        check_vma=False,
    )
```

```python
import jax
import jax.numpy as jnp
from jax import lax
from jax.sharding import PartitionSpec as P

LEVELS = 64


epsilon = 1e-05
sigma_weight = 2.0


def rms_scale(values):
    squares = jnp.mean(values * values, axis=-1, keepdims=True)
    return lax.rsqrt(squares + epsilon)


def lookup_rows(row_ids, embed_table):
    vocab_size = embed_table.shape[0]
    column = jnp.arange(vocab_size, dtype=jnp.int32)
    onehot = (row_ids[:, None] == column[None, :]).astype(jnp.bfloat16)
    return jnp.dot(onehot, embed_table, preferred_element_type=jnp.float32).astype(jnp.bfloat16)


def picked_logprob(logprob, targets):
    vocab_size = logprob.shape[-1]
    column = jnp.arange(vocab_size, dtype=jnp.int32)
    return jnp.sum(jnp.where(column[None, :] == targets[:, None], logprob, 0.0), axis=-1)


def shifted(x, axis, size, by):
    return lax.ppermute(x, axis, [(i, (i + by) % size) for i in range(size)])


def fsdp_moved(x, mapping):
    return lax.ppermute(x, "fsdp", [(f, mapping(f)) for f in range(16)])


def ring_scatter(blocks, me, size, move):
    half = blocks.shape[-1] // 2
    ahead = blocks[..., :half]
    behind = blocks[..., half:]
    cur_a = lax.dynamic_index_in_dim(ahead, (me - 1) % size, 0, keepdims=False)
    cur_b = lax.dynamic_index_in_dim(behind, (me + 1) % size, 0, keepdims=False)
    for step in range(size - 1):
        got_a = move(cur_a, 1)
        got_b = move(cur_b, -1)
        cur_a = got_a + lax.dynamic_index_in_dim(ahead, (me - step - 2) % size, 0, keepdims=False)
        cur_b = got_b + lax.dynamic_index_in_dim(behind, (me + step + 2) % size, 0, keepdims=False)
    return jnp.concatenate([cur_a, cur_b], axis=-1)


def pair_scatter(blocks, axis_pos, me, move):
    keep = lax.dynamic_index_in_dim(blocks, me, axis_pos, keepdims=False)
    send = lax.dynamic_index_in_dim(blocks, 1 - me, axis_pos, keepdims=False)
    return keep + move(send)


def gradient_scatter(first, second):
    rows, cols = first.shape
    seg = lax.axis_index("segment")
    f = lax.axis_index("fsdp")
    rep = lax.axis_index("rep")
    y_pos = f // 4
    zh_pos = (f // 2) % 2
    core_pos = f % 2
    along_x = lambda v, by: shifted(v, "segment", 4, by)
    along_y = lambda v, by: fsdp_moved(v, lambda g: ((g // 4 + by) % 4) * 4 + g % 4)
    along_core = lambda v: fsdp_moved(v, lambda g: g ^ 1)
    along_zh = lambda v: fsdp_moved(v, lambda g: g ^ 2)
    along_zl = lambda v: shifted(v, "rep", 2, 1)
    x_near = lambda v: lax.ppermute(v, "segment", [(i, i ^ 1) for i in range(4)])
    x_far = lambda v: lax.ppermute(v, "segment", [(i, i ^ 2) for i in range(4)])
    y_near = lambda v: fsdp_moved(v, lambda g: g ^ 4)
    y_far = lambda v: fsdp_moved(v, lambda g: g ^ 8)
    both = jnp.stack([first, second]).reshape(2, 4, 4, 2, 2, 2, rows // 128, cols)
    both = pair_scatter(both, 4, core_pos, along_core)
    outs = []
    for order in (0, 1):
        blocks = both[order]
        if order == 0:
            blocks = ring_scatter(blocks, seg, 4, along_x)
            blocks = blocks.reshape((2, 2) + blocks.shape[1:])
            blocks = pair_scatter(blocks, 1, y_pos % 2, y_near)
            blocks = pair_scatter(blocks, 0, y_pos // 2, y_far)
        else:
            blocks = jnp.swapaxes(blocks, 0, 1)
            blocks = ring_scatter(blocks, y_pos, 4, along_y)
            blocks = blocks.reshape((2, 2) + blocks.shape[1:])
            blocks = pair_scatter(blocks, 1, seg % 2, x_near)
            blocks = pair_scatter(blocks, 0, seg // 2, x_far)
        outs.append(blocks)
    both = jnp.stack(outs)
    both = pair_scatter(both, 2, rep, along_zl)
    both = pair_scatter(both, 1, zh_pos, along_zh)
    outs = [both[0], both[1]]
    return outs


def on_device(
    token_ids,
    seq_lengths,
    quant_scores,
    embed_table,
    prior_weight,
    prior_gain,
    final_gain,
    head_weight,
    agent_down,
    agent_up,
):
    segments = lax.axis_size("segment")
    replicas = lax.axis_size("rep")
    segment_pos = lax.axis_index("segment")
    rep_pos = lax.axis_index("rep")
    group_seqs, seq_len = token_ids.shape
    model_width = embed_table.shape[1]
    vocab_size = embed_table.shape[0]
    half_width = prior_weight.shape[2]
    per_device = group_seqs // (segments * replicas)
    micro_count = 8
    total_rows = group_seqs * seq_len
    block_rows = total_rows // micro_count
    tick_count = micro_count + 2 * (segments - 1)
    flat_ids = token_ids.reshape(-1)
    weight_local = prior_weight[0]
    gain_local = prior_gain[0]
    is_first = segment_pos == 0
    is_last = segment_pos == segments - 1
    own_first = rep_pos == 0

    down_full, up_full = (
        lax.all_gather(agent_down, "fsdp", axis=0, tiled=True),
        lax.all_gather(agent_up, "fsdp", axis=0, tiled=True),
    )

    def apply_segment(current):
        wide_rows = current.astype(jnp.float32)
        normed = (wide_rows * rms_scale(wide_rows) * gain_local).astype(jnp.bfloat16)
        update = jnp.dot(normed, weight_local, preferred_element_type=jnp.float32)
        own_half = lax.dynamic_slice_in_dim(wide_rows, rep_pos * half_width, half_width, 1)
        return (own_half + update).astype(jnp.bfloat16)

    embedded_all = lookup_rows(flat_ids, embed_table)

    def tick_whole(tick_pos, state):
        arrived, computed, stored = state
        partner = shifted(arrived, "rep", replicas, 1)
        passed = lax.ppermute(computed, "segment", [(i, i + 1) for i in range(segments - 1)])
        micro_pos = tick_pos - 2 * segment_pos
        active = (micro_pos >= 0) & (micro_pos < micro_count)
        slot_pos = jnp.clip(micro_pos, 0, micro_count - 1)
        embedded = lax.dynamic_slice_in_dim(embedded_all, slot_pos * block_rows, block_rows, 0)
        low = jnp.where(own_first, arrived, partner)
        high = jnp.where(own_first, partner, arrived)
        joined = jnp.concatenate([low, high], axis=1)
        current = jnp.where(is_first, embedded, joined)
        result = apply_segment(current)
        previous = lax.dynamic_slice_in_dim(stored, slot_pos * block_rows, block_rows, 0)
        chosen = jnp.where(active & is_last, result, previous)
        stored = lax.dynamic_update_slice_in_dim(stored, chosen, slot_pos * block_rows, 0)
        return (passed, result, stored)

    initial = (
        jnp.zeros((block_rows, half_width), jnp.bfloat16),
        jnp.zeros((block_rows, half_width), jnp.bfloat16),
        jnp.zeros((total_rows, half_width), jnp.bfloat16),
    )
    final_half = lax.fori_loop(0, tick_count, tick_whole, initial)[2]

    positions = jnp.arange(seq_len, dtype=jnp.int32)
    next_ids = jnp.concatenate([token_ids[:, 1:], token_ids[:, :1]], axis=1)
    live_mask = (positions[None, :] < seq_lengths[:, None] - 1).astype(jnp.float32)
    counts = (seq_lengths - 1).astype(jnp.float32)

    wide_half = final_half.astype(jnp.float32)
    own_squares = jnp.sum(wide_half * wide_half, axis=-1, keepdims=True)
    squares = own_squares + shifted(own_squares, "rep", replicas, 1)
    final_scale = lax.rsqrt(squares / model_width + epsilon)
    gain_half = lax.dynamic_slice_in_dim(final_gain, rep_pos * half_width, half_width, 0)
    head_half = lax.dynamic_slice_in_dim(head_weight, rep_pos * half_width, half_width, 0)
    prior_half = (wide_half * final_scale * gain_half).astype(jnp.bfloat16)
    own_logits = jnp.dot(prior_half, head_half, preferred_element_type=jnp.float32)
    prior_logits = own_logits + shifted(own_logits, "rep", replicas, 1)
    prior_logp = jax.nn.log_softmax(prior_logits, axis=-1)
    token_terms = picked_logprob(prior_logp, next_ids.reshape(-1)).reshape(group_seqs, seq_len)
    prior_group = jnp.sum(token_terms * live_mask, axis=1) / counts
    from_last = prior_group
    for by in range(1, segments):
        moved = shifted(prior_group, "segment", segments, by)
        from_last = jnp.where((segment_pos - by) % segments == segments - 1, moved, from_last)
    prior_group = from_last

    own_seq = (segment_pos * replicas + rep_pos) * per_device
    prior_mine = lax.dynamic_slice_in_dim(prior_group, own_seq, per_device, 0)
    mine_ids = lax.dynamic_slice_in_dim(token_ids, own_seq, per_device, 0).reshape(-1)
    mine_next = lax.dynamic_slice_in_dim(next_ids, own_seq, per_device, 0).reshape(-1)
    mine_live = lax.dynamic_slice_in_dim(live_mask, own_seq, per_device, 0)
    mine_counts = lax.dynamic_slice_in_dim(counts, own_seq, per_device, 0)
    mine_scores = lax.dynamic_slice_in_dim(quant_scores, own_seq, per_device, 0)
    start_wide = lookup_rows(mine_ids, embed_table).astype(jnp.float32)
    unit_rows = (start_wide * rms_scale(start_wide)).astype(jnp.bfloat16)
    latent = jnp.dot(unit_rows, down_full, preferred_element_type=jnp.float32).astype(jnp.bfloat16)
    hidden = start_wide + lax.dot_general(
        latent, up_full, (((1,), (1,)), ((), ())), preferred_element_type=jnp.float32
    )
    inverse = rms_scale(hidden)
    agent_final = (hidden * inverse * final_gain).astype(jnp.bfloat16)
    logprob = jax.nn.log_softmax(
        jnp.dot(agent_final, head_weight, preferred_element_type=jnp.float32), axis=-1
    )
    agent_ll = (
        jnp.sum(picked_logprob(logprob, mine_next).reshape(per_device, seq_len) * mine_live, axis=1)
        / mine_counts
    )
    margin = prior_mine + sigma_weight * mine_scores.astype(jnp.float32) / LEVELS - agent_ll
    row_factor = ((2.0 * margin / mine_counts)[:, None] * mine_live).reshape(-1)
    column = jnp.arange(vocab_size, dtype=jnp.int32)
    onehot_next = (mine_next[:, None] == column[None, :]).astype(jnp.float32)
    logit_grad = (row_factor[:, None] * (jnp.exp(logprob) - onehot_next)).astype(jnp.bfloat16)
    scaled_grad = (
        lax.dot_general(
            logit_grad, head_weight, (((1,), (1,)), ((), ())), preferred_element_type=jnp.float32
        )
        * final_gain
    )
    hidden_grad = (
        inverse * scaled_grad
        - hidden
        * inverse
        * inverse
        * inverse
        * jnp.mean(hidden * scaled_grad, axis=-1, keepdims=True)
    ).astype(jnp.bfloat16)
    up_grad = lax.dot_general(
        hidden_grad, latent, (((0,), (0,)), ((), ())), preferred_element_type=jnp.float32
    )
    latent_grad = jnp.dot(hidden_grad, up_full, preferred_element_type=jnp.float32).astype(
        jnp.bfloat16
    )
    down_grad = lax.dot_general(
        unit_rows, latent_grad, (((0,), (0,)), ((), ())), preferred_element_type=jnp.float32
    )
    down_share, up_share = gradient_scatter(down_grad, up_grad)
    return (down_share, up_share)


def solution(mesh):
    placed = (
        P("fsdp", None),
        P("fsdp"),
        P("fsdp"),
        P(),
        P("segment", None, "rep"),
        P("segment", None),
        P(),
        P(),
        P("fsdp", None),
        P("fsdp", None),
    )
    return jax.shard_map(
        on_device,
        mesh=mesh,
        in_specs=placed,
        out_specs=(P(("segment", "fsdp", "rep"), None), P(("segment", "fsdp", "rep"), None)),
        check_vma=False,
    )
```

```python
import jax
import jax.numpy as jnp
from jax import lax
from jax.sharding import PartitionSpec as P

LEVELS = 64


epsilon = 1e-05
sigma_weight = 2.0


def rms_scale(values):
    squares = jnp.mean(values * values, axis=-1, keepdims=True)
    return lax.rsqrt(squares + epsilon)


def lookup_rows(row_ids, embed_table):
    vocab_size = embed_table.shape[0]
    column = jnp.arange(vocab_size, dtype=jnp.int32)
    onehot = (row_ids[:, None] == column[None, :]).astype(jnp.bfloat16)
    return jnp.dot(onehot, embed_table, preferred_element_type=jnp.float32).astype(jnp.bfloat16)


def picked_logprob(logprob, targets):
    vocab_size = logprob.shape[-1]
    column = jnp.arange(vocab_size, dtype=jnp.int32)
    return jnp.sum(jnp.where(column[None, :] == targets[:, None], logprob, 0.0), axis=-1)


def shifted(x, axis, size, by):
    return lax.ppermute(x, axis, [(i, (i + by) % size) for i in range(size)])


def fsdp_moved(x, mapping):
    return lax.ppermute(x, "fsdp", [(f, mapping(f)) for f in range(16)])


def ring_scatter(blocks, me, size, move):
    half = blocks.shape[-1] // 2
    ahead = blocks[..., :half]
    behind = blocks[..., half:]
    cur_a = lax.dynamic_index_in_dim(ahead, (me - 1) % size, 0, keepdims=False)
    cur_b = lax.dynamic_index_in_dim(behind, (me + 1) % size, 0, keepdims=False)
    for step in range(size - 1):
        got_a = move(cur_a, 1)
        got_b = move(cur_b, -1)
        cur_a = got_a + lax.dynamic_index_in_dim(ahead, (me - step - 2) % size, 0, keepdims=False)
        cur_b = got_b + lax.dynamic_index_in_dim(behind, (me + step + 2) % size, 0, keepdims=False)
    return jnp.concatenate([cur_a, cur_b], axis=-1)


def pair_scatter(blocks, axis_pos, me, move):
    keep = lax.dynamic_index_in_dim(blocks, me, axis_pos, keepdims=False)
    send = lax.dynamic_index_in_dim(blocks, 1 - me, axis_pos, keepdims=False)
    return keep + move(send)


def gradient_scatter(first, second):
    rows, cols = first.shape
    seg = lax.axis_index("segment")
    f = lax.axis_index("fsdp")
    rep = lax.axis_index("rep")
    y_pos = f // 4
    zh_pos = (f // 2) % 2
    core_pos = f % 2
    along_x = lambda v, by: shifted(v, "segment", 4, by)
    along_y = lambda v, by: fsdp_moved(v, lambda g: ((g // 4 + by) % 4) * 4 + g % 4)
    along_core = lambda v: fsdp_moved(v, lambda g: g ^ 1)
    along_zh = lambda v: fsdp_moved(v, lambda g: g ^ 2)
    along_zl = lambda v: shifted(v, "rep", 2, 1)
    outs = []
    for grad, order in ((first, 0), (second, 1)):
        blocks = grad.reshape(4, 4, 2, 2, 2, rows // 128, cols)
        blocks = pair_scatter(blocks, 3, core_pos, along_core)
        if order == 0:
            blocks = ring_scatter(blocks, seg, 4, along_x)
            blocks = ring_scatter(blocks, y_pos, 4, along_y)
        else:
            blocks = jnp.swapaxes(blocks, 0, 1)
            blocks = ring_scatter(blocks, y_pos, 4, along_y)
            blocks = ring_scatter(blocks, seg, 4, along_x)
        outs.append(blocks)
    outs = [pair_scatter(b, 1, rep, along_zl) for b in outs]
    outs = [pair_scatter(b, 0, zh_pos, along_zh) for b in outs]
    return outs


def on_device(
    token_ids,
    seq_lengths,
    quant_scores,
    embed_table,
    prior_weight,
    prior_gain,
    final_gain,
    head_weight,
    agent_down,
    agent_up,
):
    segments = lax.axis_size("segment")
    replicas = lax.axis_size("rep")
    segment_pos = lax.axis_index("segment")
    rep_pos = lax.axis_index("rep")
    group_seqs, seq_len = token_ids.shape
    model_width = embed_table.shape[1]
    vocab_size = embed_table.shape[0]
    half_width = prior_weight.shape[2]
    per_device = group_seqs // (segments * replicas)
    micro_count = 8
    total_rows = group_seqs * seq_len
    block_rows = total_rows // micro_count
    tick_count = micro_count + 2 * (segments - 1)
    flat_ids = token_ids.reshape(-1)
    weight_local = prior_weight[0]
    gain_local = prior_gain[0]
    is_first = segment_pos == 0
    is_last = segment_pos == segments - 1
    own_first = rep_pos == 0

    down_full, up_full = (
        lax.all_gather(agent_down, "fsdp", axis=0, tiled=True),
        lax.all_gather(agent_up, "fsdp", axis=0, tiled=True),
    )

    def apply_segment(current):
        wide_rows = current.astype(jnp.float32)
        normed = (wide_rows * rms_scale(wide_rows) * gain_local).astype(jnp.bfloat16)
        update = jnp.dot(normed, weight_local, preferred_element_type=jnp.float32)
        own_half = lax.dynamic_slice_in_dim(wide_rows, rep_pos * half_width, half_width, 1)
        return (own_half + update).astype(jnp.bfloat16)

    embedded_all = lookup_rows(flat_ids, embed_table)

    def tick_whole(tick_pos, state):
        arrived, computed, stored = state
        partner = shifted(arrived, "rep", replicas, 1)
        passed = lax.ppermute(computed, "segment", [(i, i + 1) for i in range(segments - 1)])
        micro_pos = tick_pos - 2 * segment_pos
        active = (micro_pos >= 0) & (micro_pos < micro_count)
        slot_pos = jnp.clip(micro_pos, 0, micro_count - 1)
        embedded = lax.dynamic_slice_in_dim(embedded_all, slot_pos * block_rows, block_rows, 0)
        low = jnp.where(own_first, arrived, partner)
        high = jnp.where(own_first, partner, arrived)
        joined = jnp.concatenate([low, high], axis=1)
        current = jnp.where(is_first, embedded, joined)
        result = apply_segment(current)
        previous = lax.dynamic_slice_in_dim(stored, slot_pos * block_rows, block_rows, 0)
        chosen = jnp.where(active & is_last, result, previous)
        stored = lax.dynamic_update_slice_in_dim(stored, chosen, slot_pos * block_rows, 0)
        return (passed, result, stored)

    initial = (
        jnp.zeros((block_rows, half_width), jnp.bfloat16),
        jnp.zeros((block_rows, half_width), jnp.bfloat16),
        jnp.zeros((total_rows, half_width), jnp.bfloat16),
    )
    state = initial
    for tick_pos in range(tick_count):
        state = tick_whole(tick_pos, state)
    final_half = state[2]

    positions = jnp.arange(seq_len, dtype=jnp.int32)
    next_ids = jnp.concatenate([token_ids[:, 1:], token_ids[:, :1]], axis=1)
    live_mask = (positions[None, :] < seq_lengths[:, None] - 1).astype(jnp.float32)
    counts = (seq_lengths - 1).astype(jnp.float32)

    wide_half = final_half.astype(jnp.float32)
    own_squares = jnp.sum(wide_half * wide_half, axis=-1, keepdims=True)
    squares = own_squares + shifted(own_squares, "rep", replicas, 1)
    final_scale = lax.rsqrt(squares / model_width + epsilon)
    gain_half = lax.dynamic_slice_in_dim(final_gain, rep_pos * half_width, half_width, 0)
    head_half = lax.dynamic_slice_in_dim(head_weight, rep_pos * half_width, half_width, 0)
    prior_half = (wide_half * final_scale * gain_half).astype(jnp.bfloat16)
    own_logits = jnp.dot(prior_half, head_half, preferred_element_type=jnp.float32)
    prior_logits = own_logits + shifted(own_logits, "rep", replicas, 1)
    prior_logp = jax.nn.log_softmax(prior_logits, axis=-1)
    token_terms = picked_logprob(prior_logp, next_ids.reshape(-1)).reshape(group_seqs, seq_len)
    prior_group = jnp.sum(token_terms * live_mask, axis=1) / counts
    from_last = prior_group
    for by in range(1, segments):
        moved = shifted(prior_group, "segment", segments, by)
        from_last = jnp.where((segment_pos - by) % segments == segments - 1, moved, from_last)
    prior_group = from_last

    own_seq = (segment_pos * replicas + rep_pos) * per_device
    prior_mine = lax.dynamic_slice_in_dim(prior_group, own_seq, per_device, 0)
    mine_ids = lax.dynamic_slice_in_dim(token_ids, own_seq, per_device, 0).reshape(-1)
    mine_next = lax.dynamic_slice_in_dim(next_ids, own_seq, per_device, 0).reshape(-1)
    mine_live = lax.dynamic_slice_in_dim(live_mask, own_seq, per_device, 0)
    mine_counts = lax.dynamic_slice_in_dim(counts, own_seq, per_device, 0)
    mine_scores = lax.dynamic_slice_in_dim(quant_scores, own_seq, per_device, 0)
    start_wide = lookup_rows(mine_ids, embed_table).astype(jnp.float32)
    unit_rows = (start_wide * rms_scale(start_wide)).astype(jnp.bfloat16)
    latent = jnp.dot(unit_rows, down_full, preferred_element_type=jnp.float32).astype(jnp.bfloat16)
    hidden = start_wide + lax.dot_general(
        latent, up_full, (((1,), (1,)), ((), ())), preferred_element_type=jnp.float32
    )
    inverse = rms_scale(hidden)
    agent_final = (hidden * inverse * final_gain).astype(jnp.bfloat16)
    logprob = jax.nn.log_softmax(
        jnp.dot(agent_final, head_weight, preferred_element_type=jnp.float32), axis=-1
    )
    agent_ll = (
        jnp.sum(picked_logprob(logprob, mine_next).reshape(per_device, seq_len) * mine_live, axis=1)
        / mine_counts
    )
    margin = prior_mine + sigma_weight * mine_scores.astype(jnp.float32) / LEVELS - agent_ll
    row_factor = ((2.0 * margin / mine_counts)[:, None] * mine_live).reshape(-1)
    column = jnp.arange(vocab_size, dtype=jnp.int32)
    onehot_next = (mine_next[:, None] == column[None, :]).astype(jnp.float32)
    logit_grad = (row_factor[:, None] * (jnp.exp(logprob) - onehot_next)).astype(jnp.bfloat16)
    scaled_grad = (
        lax.dot_general(
            logit_grad, head_weight, (((1,), (1,)), ((), ())), preferred_element_type=jnp.float32
        )
        * final_gain
    )
    hidden_grad = (
        inverse * scaled_grad
        - hidden
        * inverse
        * inverse
        * inverse
        * jnp.mean(hidden * scaled_grad, axis=-1, keepdims=True)
    ).astype(jnp.bfloat16)
    up_grad = lax.dot_general(
        hidden_grad, latent, (((0,), (0,)), ((), ())), preferred_element_type=jnp.float32
    )
    latent_grad = jnp.dot(hidden_grad, up_full, preferred_element_type=jnp.float32).astype(
        jnp.bfloat16
    )
    down_grad = lax.dot_general(
        unit_rows, latent_grad, (((0,), (0,)), ((), ())), preferred_element_type=jnp.float32
    )
    down_share, up_share = gradient_scatter(down_grad, up_grad)
    return (down_share, up_share)


def solution(mesh):
    placed = (
        P("fsdp", None),
        P("fsdp"),
        P("fsdp"),
        P(),
        P("segment", None, "rep"),
        P("segment", None),
        P(),
        P(),
        P("fsdp", None),
        P("fsdp", None),
    )
    return jax.shard_map(
        on_device,
        mesh=mesh,
        in_specs=placed,
        out_specs=(P(("segment", "fsdp", "rep"), None), P(("segment", "fsdp", "rep"), None)),
        check_vma=False,
    )
```

```python
import jax
import jax.numpy as jnp
from jax import lax
from jax.sharding import PartitionSpec as P
from jax.experimental import pallas as pl
from jax.experimental.pallas import tpu as pltpu

LEVELS = 64


epsilon = 1e-05
sigma_weight = 2.0


def rms_scale(values):
    squares = jnp.mean(values * values, axis=-1, keepdims=True)
    return lax.rsqrt(squares + epsilon)


def lookup_rows(row_ids, embed_table):
    vocab_size = embed_table.shape[0]
    column = jnp.arange(vocab_size, dtype=jnp.int32)
    onehot = (row_ids[:, None] == column[None, :]).astype(jnp.bfloat16)
    return jnp.dot(onehot, embed_table, preferred_element_type=jnp.float32).astype(jnp.bfloat16)


def picked_logprob(logprob, targets):
    vocab_size = logprob.shape[-1]
    column = jnp.arange(vocab_size, dtype=jnp.int32)
    return jnp.sum(jnp.where(column[None, :] == targets[:, None], logprob, 0.0), axis=-1)


def stage_kernel(normed_ref, weight_ref, own_ref, out_ref):
    update = jnp.dot(normed_ref[...], weight_ref[...], preferred_element_type=jnp.float32)
    out_ref[...] = (own_ref[...].astype(jnp.float32) + update).astype(out_ref.dtype)


def stage_product(normed, weight, own):
    rows, depth = normed.shape
    width = weight.shape[1]
    tile = min(width, 256)
    return pl.pallas_call(
        stage_kernel,
        grid=(width // tile,),
        in_specs=[
            pl.BlockSpec((rows, depth), lambda j: (0, 0)),
            pl.BlockSpec((depth, tile), lambda j: (0, j)),
            pl.BlockSpec((rows, tile), lambda j: (0, j)),
        ],
        out_specs=pl.BlockSpec((rows, tile), lambda j: (0, j)),
        out_shape=jax.ShapeDtypeStruct((rows, width), jnp.bfloat16),
        compiler_params=pltpu.CompilerParams(vmem_limit_bytes=32 * 1024 * 1024),
    )(normed, weight, own)


def shifted(x, axis, size, by):
    return lax.ppermute(x, axis, [(i, (i + by) % size) for i in range(size)])


def fsdp_moved(x, mapping):
    return lax.ppermute(x, "fsdp", [(f, mapping(f)) for f in range(16)])


def ring_scatter(blocks, me, size, move):
    half = blocks.shape[-1] // 2
    ahead = blocks[..., :half]
    behind = blocks[..., half:]
    cur_a = lax.dynamic_index_in_dim(ahead, (me - 1) % size, 0, keepdims=False)
    cur_b = lax.dynamic_index_in_dim(behind, (me + 1) % size, 0, keepdims=False)
    for step in range(size - 1):
        got_a = move(cur_a, 1)
        got_b = move(cur_b, -1)
        cur_a = got_a + lax.dynamic_index_in_dim(ahead, (me - step - 2) % size, 0, keepdims=False)
        cur_b = got_b + lax.dynamic_index_in_dim(behind, (me + step + 2) % size, 0, keepdims=False)
    return jnp.concatenate([cur_a, cur_b], axis=-1)


def pair_scatter(blocks, axis_pos, me, move):
    keep = lax.dynamic_index_in_dim(blocks, me, axis_pos, keepdims=False)
    send = lax.dynamic_index_in_dim(blocks, 1 - me, axis_pos, keepdims=False)
    return keep + move(send)


def gradient_scatter(first, second):
    rows, cols = first.shape
    seg = lax.axis_index("segment")
    f = lax.axis_index("fsdp")
    rep = lax.axis_index("rep")
    y_pos = f // 4
    zh_pos = (f // 2) % 2
    core_pos = f % 2
    along_x = lambda v, by: shifted(v, "segment", 4, by)
    along_y = lambda v, by: fsdp_moved(v, lambda g: ((g // 4 + by) % 4) * 4 + g % 4)
    along_core = lambda v: fsdp_moved(v, lambda g: g ^ 1)
    along_zh = lambda v: fsdp_moved(v, lambda g: g ^ 2)
    along_zl = lambda v: shifted(v, "rep", 2, 1)
    outs = []
    for grad, order in ((first, 0), (second, 1)):
        blocks = grad.reshape(4, 4, 2, 2, 2, rows // 128, cols)
        blocks = pair_scatter(blocks, 3, core_pos, along_core)
        if order == 0:
            blocks = ring_scatter(blocks, seg, 4, along_x)
            blocks = ring_scatter(blocks, y_pos, 4, along_y)
        else:
            blocks = jnp.swapaxes(blocks, 0, 1)
            blocks = ring_scatter(blocks, y_pos, 4, along_y)
            blocks = ring_scatter(blocks, seg, 4, along_x)
        outs.append(blocks)
    outs = [pair_scatter(b, 1, rep, along_zl) for b in outs]
    outs = [pair_scatter(b, 0, zh_pos, along_zh) for b in outs]
    return outs


def on_device(
    token_ids,
    seq_lengths,
    quant_scores,
    embed_table,
    prior_weight,
    prior_gain,
    final_gain,
    head_weight,
    agent_down,
    agent_up,
):
    segments = lax.axis_size("segment")
    replicas = lax.axis_size("rep")
    segment_pos = lax.axis_index("segment")
    rep_pos = lax.axis_index("rep")
    group_seqs, seq_len = token_ids.shape
    model_width = embed_table.shape[1]
    vocab_size = embed_table.shape[0]
    half_width = prior_weight.shape[2]
    per_device = group_seqs // (segments * replicas)
    micro_count = 8
    total_rows = group_seqs * seq_len
    block_rows = total_rows // micro_count
    tick_count = micro_count + 2 * (segments - 1)
    flat_ids = token_ids.reshape(-1)
    weight_local = prior_weight[0]
    gain_local = prior_gain[0]
    is_first = segment_pos == 0
    is_last = segment_pos == segments - 1
    own_first = rep_pos == 0

    down_full, up_full = (
        lax.all_gather(agent_down, "fsdp", axis=0, tiled=True),
        lax.all_gather(agent_up, "fsdp", axis=0, tiled=True),
    )

    def apply_segment(current):
        wide_rows = current.astype(jnp.float32)
        normed = (wide_rows * rms_scale(wide_rows) * gain_local).astype(jnp.bfloat16)
        own_half = lax.dynamic_slice_in_dim(current, rep_pos * half_width, half_width, 1)
        return stage_product(normed, weight_local, own_half)

    embedded_all = lookup_rows(flat_ids, embed_table)

    def tick_whole(tick_pos, state):
        arrived, computed, stored = state
        partner = shifted(arrived, "rep", replicas, 1)
        passed = lax.ppermute(computed, "segment", [(i, i + 1) for i in range(segments - 1)])
        micro_pos = tick_pos - 2 * segment_pos
        active = (micro_pos >= 0) & (micro_pos < micro_count)
        slot_pos = jnp.clip(micro_pos, 0, micro_count - 1)
        embedded = lax.dynamic_slice_in_dim(embedded_all, slot_pos * block_rows, block_rows, 0)
        low = jnp.where(own_first, arrived, partner)
        high = jnp.where(own_first, partner, arrived)
        joined = jnp.concatenate([low, high], axis=1)
        current = jnp.where(is_first, embedded, joined)
        result = apply_segment(current)
        previous = lax.dynamic_slice_in_dim(stored, slot_pos * block_rows, block_rows, 0)
        chosen = jnp.where(active & is_last, result, previous)
        stored = lax.dynamic_update_slice_in_dim(stored, chosen, slot_pos * block_rows, 0)
        return (passed, result, stored)

    initial = (
        jnp.zeros((block_rows, half_width), jnp.bfloat16),
        jnp.zeros((block_rows, half_width), jnp.bfloat16),
        jnp.zeros((total_rows, half_width), jnp.bfloat16),
    )
    final_half = lax.fori_loop(0, tick_count, tick_whole, initial)[2]

    positions = jnp.arange(seq_len, dtype=jnp.int32)
    next_ids = jnp.concatenate([token_ids[:, 1:], token_ids[:, :1]], axis=1)
    live_mask = (positions[None, :] < seq_lengths[:, None] - 1).astype(jnp.float32)
    counts = (seq_lengths - 1).astype(jnp.float32)

    wide_half = final_half.astype(jnp.float32)
    own_squares = jnp.sum(wide_half * wide_half, axis=-1, keepdims=True)
    squares = own_squares + shifted(own_squares, "rep", replicas, 1)
    final_scale = lax.rsqrt(squares / model_width + epsilon)
    gain_half = lax.dynamic_slice_in_dim(final_gain, rep_pos * half_width, half_width, 0)
    head_half = lax.dynamic_slice_in_dim(head_weight, rep_pos * half_width, half_width, 0)
    prior_half = (wide_half * final_scale * gain_half).astype(jnp.bfloat16)
    own_logits = jnp.dot(prior_half, head_half, preferred_element_type=jnp.float32)
    prior_logits = own_logits + shifted(own_logits, "rep", replicas, 1)
    prior_logp = jax.nn.log_softmax(prior_logits, axis=-1)
    token_terms = picked_logprob(prior_logp, next_ids.reshape(-1)).reshape(group_seqs, seq_len)
    prior_group = jnp.sum(token_terms * live_mask, axis=1) / counts
    from_last = prior_group
    for by in range(1, segments):
        moved = shifted(prior_group, "segment", segments, by)
        from_last = jnp.where((segment_pos - by) % segments == segments - 1, moved, from_last)
    prior_group = from_last

    own_seq = (segment_pos * replicas + rep_pos) * per_device
    prior_mine = lax.dynamic_slice_in_dim(prior_group, own_seq, per_device, 0)
    mine_ids = lax.dynamic_slice_in_dim(token_ids, own_seq, per_device, 0).reshape(-1)
    mine_next = lax.dynamic_slice_in_dim(next_ids, own_seq, per_device, 0).reshape(-1)
    mine_live = lax.dynamic_slice_in_dim(live_mask, own_seq, per_device, 0)
    mine_counts = lax.dynamic_slice_in_dim(counts, own_seq, per_device, 0)
    mine_scores = lax.dynamic_slice_in_dim(quant_scores, own_seq, per_device, 0)
    start_wide = lookup_rows(mine_ids, embed_table).astype(jnp.float32)
    unit_rows = (start_wide * rms_scale(start_wide)).astype(jnp.bfloat16)
    latent = jnp.dot(unit_rows, down_full, preferred_element_type=jnp.float32).astype(jnp.bfloat16)
    hidden = start_wide + lax.dot_general(
        latent, up_full, (((1,), (1,)), ((), ())), preferred_element_type=jnp.float32
    )
    inverse = rms_scale(hidden)
    agent_final = (hidden * inverse * final_gain).astype(jnp.bfloat16)
    logprob = jax.nn.log_softmax(
        jnp.dot(agent_final, head_weight, preferred_element_type=jnp.float32), axis=-1
    )
    agent_ll = (
        jnp.sum(picked_logprob(logprob, mine_next).reshape(per_device, seq_len) * mine_live, axis=1)
        / mine_counts
    )
    margin = prior_mine + sigma_weight * mine_scores.astype(jnp.float32) / LEVELS - agent_ll
    row_factor = ((2.0 * margin / mine_counts)[:, None] * mine_live).reshape(-1)
    column = jnp.arange(vocab_size, dtype=jnp.int32)
    onehot_next = (mine_next[:, None] == column[None, :]).astype(jnp.float32)
    logit_grad = (row_factor[:, None] * (jnp.exp(logprob) - onehot_next)).astype(jnp.bfloat16)
    scaled_grad = (
        lax.dot_general(
            logit_grad, head_weight, (((1,), (1,)), ((), ())), preferred_element_type=jnp.float32
        )
        * final_gain
    )
    hidden_grad = (
        inverse * scaled_grad
        - hidden
        * inverse
        * inverse
        * inverse
        * jnp.mean(hidden * scaled_grad, axis=-1, keepdims=True)
    ).astype(jnp.bfloat16)
    up_grad = lax.dot_general(
        hidden_grad, latent, (((0,), (0,)), ((), ())), preferred_element_type=jnp.float32
    )
    latent_grad = jnp.dot(hidden_grad, up_full, preferred_element_type=jnp.float32).astype(
        jnp.bfloat16
    )
    down_grad = lax.dot_general(
        unit_rows, latent_grad, (((0,), (0,)), ((), ())), preferred_element_type=jnp.float32
    )
    down_share, up_share = gradient_scatter(down_grad, up_grad)
    return (down_share, up_share)


def solution(mesh):
    placed = (
        P("fsdp", None),
        P("fsdp"),
        P("fsdp"),
        P(),
        P("segment", None, "rep"),
        P("segment", None),
        P(),
        P(),
        P("fsdp", None),
        P("fsdp", None),
    )
    return jax.shard_map(
        on_device,
        mesh=mesh,
        in_specs=placed,
        out_specs=(P(("segment", "fsdp", "rep"), None), P(("segment", "fsdp", "rep"), None)),
        check_vma=False,
    )
```

```python
import jax
import jax.numpy as jnp
from jax import lax
from jax.sharding import PartitionSpec as P

LEVELS = 64


epsilon = 1e-05
sigma_weight = 2.0


def rms_scale(values):
    squares = jnp.mean(values * values, axis=-1, keepdims=True)
    return lax.rsqrt(squares + epsilon)


def lookup_rows(row_ids, embed_table):
    vocab_size = embed_table.shape[0]
    column = jnp.arange(vocab_size, dtype=jnp.int32)
    onehot = (row_ids[:, None] == column[None, :]).astype(jnp.bfloat16)
    return jnp.dot(onehot, embed_table, preferred_element_type=jnp.float32).astype(jnp.bfloat16)


def picked_logprob(logprob, targets):
    vocab_size = logprob.shape[-1]
    column = jnp.arange(vocab_size, dtype=jnp.int32)
    return jnp.sum(jnp.where(column[None, :] == targets[:, None], logprob, 0.0), axis=-1)


def shifted(x, axis, size, by):
    return lax.ppermute(x, axis, [(i, (i + by) % size) for i in range(size)])


def fsdp_moved(x, mapping):
    return lax.ppermute(x, "fsdp", [(f, mapping(f)) for f in range(16)])


def ring_scatter(blocks, me, size, move):
    half = blocks.shape[-1] // 2
    ahead = blocks[..., :half]
    behind = blocks[..., half:]
    cur_a = lax.dynamic_index_in_dim(ahead, (me - 1) % size, 0, keepdims=False)
    cur_b = lax.dynamic_index_in_dim(behind, (me + 1) % size, 0, keepdims=False)
    for step in range(size - 1):
        got_a = move(cur_a, 1)
        got_b = move(cur_b, -1)
        cur_a = got_a + lax.dynamic_index_in_dim(ahead, (me - step - 2) % size, 0, keepdims=False)
        cur_b = got_b + lax.dynamic_index_in_dim(behind, (me + step + 2) % size, 0, keepdims=False)
    return jnp.concatenate([cur_a, cur_b], axis=-1)


def pair_scatter(blocks, axis_pos, me, move):
    keep = lax.dynamic_index_in_dim(blocks, me, axis_pos, keepdims=False)
    send = lax.dynamic_index_in_dim(blocks, 1 - me, axis_pos, keepdims=False)
    return keep + move(send)


def gradient_scatter(first, second):
    rows, cols = first.shape
    seg = lax.axis_index("segment")
    f = lax.axis_index("fsdp")
    rep = lax.axis_index("rep")
    y_pos = f // 4
    zh_pos = (f // 2) % 2
    core_pos = f % 2
    along_x = lambda v, by: shifted(v, "segment", 4, by)
    along_y = lambda v, by: fsdp_moved(v, lambda g: ((g // 4 + by) % 4) * 4 + g % 4)
    along_core = lambda v: fsdp_moved(v, lambda g: g ^ 1)
    along_zh = lambda v: fsdp_moved(v, lambda g: g ^ 2)
    along_zl = lambda v: shifted(v, "rep", 2, 1)
    outs = []
    for grad, order in ((first, 0), (second, 1)):
        blocks = grad.reshape(4, 4, 2, 2, 2, rows // 128, cols)
        blocks = pair_scatter(blocks, 3, core_pos, along_core)
        if order == 0:
            blocks = ring_scatter(blocks, seg, 4, along_x)
            blocks = ring_scatter(blocks, y_pos, 4, along_y)
        else:
            blocks = jnp.swapaxes(blocks, 0, 1)
            blocks = ring_scatter(blocks, y_pos, 4, along_y)
            blocks = ring_scatter(blocks, seg, 4, along_x)
        outs.append(blocks)
    outs = [pair_scatter(b, 1, rep, along_zl) for b in outs]
    outs = [pair_scatter(b, 0, zh_pos, along_zh) for b in outs]
    return outs


def on_device(
    token_ids,
    seq_lengths,
    quant_scores,
    embed_table,
    prior_weight,
    prior_gain,
    final_gain,
    head_weight,
    agent_down,
    agent_up,
):
    segments = lax.axis_size("segment")
    replicas = lax.axis_size("rep")
    segment_pos = lax.axis_index("segment")
    rep_pos = lax.axis_index("rep")
    group_seqs, seq_len = token_ids.shape
    model_width = embed_table.shape[1]
    vocab_size = embed_table.shape[0]
    half_width = prior_weight.shape[2]
    per_device = group_seqs // (segments * replicas)
    micro_count = 8
    total_rows = group_seqs * seq_len
    block_rows = total_rows // micro_count
    tick_count = micro_count + 3 * (segments - 1)
    flat_ids = token_ids.reshape(-1)
    weight_local = prior_weight[0]
    gain_local = prior_gain[0]
    is_first = segment_pos == 0
    is_last = segment_pos == segments - 1
    own_first = rep_pos == 0

    down_full, up_full = (
        lax.all_gather(agent_down, "fsdp", axis=0, tiled=True),
        lax.all_gather(agent_up, "fsdp", axis=0, tiled=True),
    )

    def apply_segment(current):
        wide_rows = current.astype(jnp.float32)
        normed = (wide_rows * rms_scale(wide_rows) * gain_local).astype(jnp.bfloat16)
        update = jnp.dot(normed, weight_local, preferred_element_type=jnp.float32)
        own_half = lax.dynamic_slice_in_dim(wide_rows, rep_pos * half_width, half_width, 1)
        return (own_half + update).astype(jnp.bfloat16)

    embedded_all = lookup_rows(flat_ids, embed_table)

    def tick_whole(tick_pos, state):
        arrived, own_prev, partner_prev, computed, stored = state
        partner = shifted(arrived, "rep", replicas, 1)
        passed = lax.ppermute(computed, "segment", [(i, i + 1) for i in range(segments - 1)])
        micro_pos = tick_pos - 3 * segment_pos
        active = (micro_pos >= 0) & (micro_pos < micro_count)
        slot_pos = jnp.clip(micro_pos, 0, micro_count - 1)
        embedded = lax.dynamic_slice_in_dim(embedded_all, slot_pos * block_rows, block_rows, 0)
        low = jnp.where(own_first, own_prev, partner_prev)
        high = jnp.where(own_first, partner_prev, own_prev)
        joined = jnp.concatenate([low, high], axis=1)
        current = jnp.where(is_first, embedded, joined)
        result = apply_segment(current)
        previous = lax.dynamic_slice_in_dim(stored, slot_pos * block_rows, block_rows, 0)
        chosen = jnp.where(active & is_last, result, previous)
        stored = lax.dynamic_update_slice_in_dim(stored, chosen, slot_pos * block_rows, 0)
        return (passed, arrived, partner, result, stored)

    initial = (
        jnp.zeros((block_rows, half_width), jnp.bfloat16),
        jnp.zeros((block_rows, half_width), jnp.bfloat16),
        jnp.zeros((block_rows, half_width), jnp.bfloat16),
        jnp.zeros((block_rows, half_width), jnp.bfloat16),
        jnp.zeros((total_rows, half_width), jnp.bfloat16),
    )
    final_half = lax.fori_loop(0, tick_count, tick_whole, initial)[4]

    positions = jnp.arange(seq_len, dtype=jnp.int32)
    next_ids = jnp.concatenate([token_ids[:, 1:], token_ids[:, :1]], axis=1)
    live_mask = (positions[None, :] < seq_lengths[:, None] - 1).astype(jnp.float32)
    counts = (seq_lengths - 1).astype(jnp.float32)

    wide_half = final_half.astype(jnp.float32)
    own_squares = jnp.sum(wide_half * wide_half, axis=-1, keepdims=True)
    squares = own_squares + shifted(own_squares, "rep", replicas, 1)
    final_scale = lax.rsqrt(squares / model_width + epsilon)
    gain_half = lax.dynamic_slice_in_dim(final_gain, rep_pos * half_width, half_width, 0)
    head_half = lax.dynamic_slice_in_dim(head_weight, rep_pos * half_width, half_width, 0)
    prior_half = (wide_half * final_scale * gain_half).astype(jnp.bfloat16)
    own_logits = jnp.dot(prior_half, head_half, preferred_element_type=jnp.float32)
    prior_logits = own_logits + shifted(own_logits, "rep", replicas, 1)
    prior_logp = jax.nn.log_softmax(prior_logits, axis=-1)
    token_terms = picked_logprob(prior_logp, next_ids.reshape(-1)).reshape(group_seqs, seq_len)
    prior_group = jnp.sum(token_terms * live_mask, axis=1) / counts
    from_last = prior_group
    for by in range(1, segments):
        moved = shifted(prior_group, "segment", segments, by)
        from_last = jnp.where((segment_pos - by) % segments == segments - 1, moved, from_last)
    prior_group = from_last

    own_seq = (segment_pos * replicas + rep_pos) * per_device
    prior_mine = lax.dynamic_slice_in_dim(prior_group, own_seq, per_device, 0)
    mine_ids = lax.dynamic_slice_in_dim(token_ids, own_seq, per_device, 0).reshape(-1)
    mine_next = lax.dynamic_slice_in_dim(next_ids, own_seq, per_device, 0).reshape(-1)
    mine_live = lax.dynamic_slice_in_dim(live_mask, own_seq, per_device, 0)
    mine_counts = lax.dynamic_slice_in_dim(counts, own_seq, per_device, 0)
    mine_scores = lax.dynamic_slice_in_dim(quant_scores, own_seq, per_device, 0)
    start_wide = lookup_rows(mine_ids, embed_table).astype(jnp.float32)
    unit_rows = (start_wide * rms_scale(start_wide)).astype(jnp.bfloat16)
    latent = jnp.dot(unit_rows, down_full, preferred_element_type=jnp.float32).astype(jnp.bfloat16)
    hidden = start_wide + lax.dot_general(
        latent, up_full, (((1,), (1,)), ((), ())), preferred_element_type=jnp.float32
    )
    inverse = rms_scale(hidden)
    agent_final = (hidden * inverse * final_gain).astype(jnp.bfloat16)
    logprob = jax.nn.log_softmax(
        jnp.dot(agent_final, head_weight, preferred_element_type=jnp.float32), axis=-1
    )
    agent_ll = (
        jnp.sum(picked_logprob(logprob, mine_next).reshape(per_device, seq_len) * mine_live, axis=1)
        / mine_counts
    )
    margin = prior_mine + sigma_weight * mine_scores.astype(jnp.float32) / LEVELS - agent_ll
    row_factor = ((2.0 * margin / mine_counts)[:, None] * mine_live).reshape(-1)
    column = jnp.arange(vocab_size, dtype=jnp.int32)
    onehot_next = (mine_next[:, None] == column[None, :]).astype(jnp.float32)
    logit_grad = (row_factor[:, None] * (jnp.exp(logprob) - onehot_next)).astype(jnp.bfloat16)
    scaled_grad = (
        lax.dot_general(
            logit_grad, head_weight, (((1,), (1,)), ((), ())), preferred_element_type=jnp.float32
        )
        * final_gain
    )
    hidden_grad = (
        inverse * scaled_grad
        - hidden
        * inverse
        * inverse
        * inverse
        * jnp.mean(hidden * scaled_grad, axis=-1, keepdims=True)
    ).astype(jnp.bfloat16)
    up_grad = lax.dot_general(
        hidden_grad, latent, (((0,), (0,)), ((), ())), preferred_element_type=jnp.float32
    )
    latent_grad = jnp.dot(hidden_grad, up_full, preferred_element_type=jnp.float32).astype(
        jnp.bfloat16
    )
    down_grad = lax.dot_general(
        unit_rows, latent_grad, (((0,), (0,)), ((), ())), preferred_element_type=jnp.float32
    )
    down_share, up_share = gradient_scatter(down_grad, up_grad)
    return (down_share, up_share)


def solution(mesh):
    placed = (
        P("fsdp", None),
        P("fsdp"),
        P("fsdp"),
        P(),
        P("segment", None, "rep"),
        P("segment", None),
        P(),
        P(),
        P("fsdp", None),
        P("fsdp", None),
    )
    return jax.shard_map(
        on_device,
        mesh=mesh,
        in_specs=placed,
        out_specs=(P(("segment", "fsdp", "rep"), None), P(("segment", "fsdp", "rep"), None)),
        check_vma=False,
    )
```

```python
import jax
import jax.numpy as jnp
from jax import lax
from jax.sharding import PartitionSpec as P

LEVELS = 64


epsilon = 1e-05
sigma_weight = 2.0


def rms_scale(values):
    squares = jnp.mean(values * values, axis=-1, keepdims=True)
    return lax.rsqrt(squares + epsilon)


def lookup_rows(row_ids, embed_table):
    vocab_size = embed_table.shape[0]
    column = jnp.arange(vocab_size, dtype=jnp.int32)
    onehot = (row_ids[:, None] == column[None, :]).astype(jnp.bfloat16)
    return jnp.dot(onehot, embed_table, preferred_element_type=jnp.float32).astype(jnp.bfloat16)


def picked_logprob(logprob, targets):
    vocab_size = logprob.shape[-1]
    column = jnp.arange(vocab_size, dtype=jnp.int32)
    return jnp.sum(jnp.where(column[None, :] == targets[:, None], logprob, 0.0), axis=-1)


def shifted(x, axis, size, by):
    return lax.ppermute(x, axis, [(i, (i + by) % size) for i in range(size)])


def fsdp_moved(x, mapping):
    return lax.ppermute(x, "fsdp", [(f, mapping(f)) for f in range(16)])


def ring_scatter(blocks, me, size, move):
    half = blocks.shape[-1] // 2
    ahead = blocks[..., :half]
    behind = blocks[..., half:]
    cur_a = lax.dynamic_index_in_dim(ahead, (me - 1) % size, 0, keepdims=False)
    cur_b = lax.dynamic_index_in_dim(behind, (me + 1) % size, 0, keepdims=False)
    for step in range(size - 1):
        got_a = move(cur_a, 1)
        got_b = move(cur_b, -1)
        cur_a = got_a + lax.dynamic_index_in_dim(ahead, (me - step - 2) % size, 0, keepdims=False)
        cur_b = got_b + lax.dynamic_index_in_dim(behind, (me + step + 2) % size, 0, keepdims=False)
    return jnp.concatenate([cur_a, cur_b], axis=-1)


def pair_scatter(blocks, axis_pos, me, move):
    keep = lax.dynamic_index_in_dim(blocks, me, axis_pos, keepdims=False)
    send = lax.dynamic_index_in_dim(blocks, 1 - me, axis_pos, keepdims=False)
    return keep + move(send)


def gradient_scatter(first, second):
    rows, cols = first.shape
    seg = lax.axis_index("segment")
    f = lax.axis_index("fsdp")
    rep = lax.axis_index("rep")
    y_pos = f // 4
    zh_pos = (f // 2) % 2
    core_pos = f % 2
    along_x = lambda v, by: shifted(v, "segment", 4, by)
    along_y = lambda v, by: fsdp_moved(v, lambda g: ((g // 4 + by) % 4) * 4 + g % 4)
    along_core = lambda v: fsdp_moved(v, lambda g: g ^ 1)
    along_zh = lambda v: fsdp_moved(v, lambda g: g ^ 2)
    along_zl = lambda v: shifted(v, "rep", 2, 1)
    outs = []
    for grad, order in ((first, 0), (second, 1)):
        blocks = grad.reshape(4, 4, 2, 2, rows // 64, cols)
        if order == 0:
            blocks = ring_scatter(blocks, seg, 4, along_x)
            blocks = ring_scatter(blocks, y_pos, 4, along_y)
        else:
            blocks = jnp.swapaxes(blocks, 0, 1)
            blocks = ring_scatter(blocks, y_pos, 4, along_y)
            blocks = ring_scatter(blocks, seg, 4, along_x)
        outs.append(blocks)
    outs = [pair_scatter(b, 1, rep, along_zl) for b in outs]
    outs = [pair_scatter(b, 0, zh_pos, along_zh) for b in outs]
    return outs


def on_device(
    token_ids,
    seq_lengths,
    quant_scores,
    embed_table,
    prior_weight,
    prior_gain,
    final_gain,
    head_weight,
    agent_down,
    agent_up,
):
    segments = lax.axis_size("segment")
    replicas = lax.axis_size("rep")
    segment_pos = lax.axis_index("segment")
    rep_pos = lax.axis_index("rep")
    group_seqs, seq_len = token_ids.shape
    model_width = embed_table.shape[1]
    vocab_size = embed_table.shape[0]
    half_width = prior_weight.shape[2]
    per_device = group_seqs // (segments * replicas)
    micro_count = 8
    total_rows = group_seqs * seq_len
    block_rows = total_rows // micro_count
    tick_count = micro_count + 2 * (segments - 1)
    flat_ids = token_ids.reshape(-1)
    weight_local = prior_weight[0]
    gain_local = prior_gain[0]
    is_first = segment_pos == 0
    is_last = segment_pos == segments - 1
    own_first = rep_pos == 0

    down_full, up_full = (
        lax.all_gather(agent_down, "fsdp", axis=0, tiled=True),
        lax.all_gather(agent_up, "fsdp", axis=0, tiled=True),
    )

    def apply_segment(current):
        wide_rows = current.astype(jnp.float32)
        normed = (wide_rows * rms_scale(wide_rows) * gain_local).astype(jnp.bfloat16)
        update = jnp.dot(normed, weight_local, preferred_element_type=jnp.float32)
        own_half = lax.dynamic_slice_in_dim(wide_rows, rep_pos * half_width, half_width, 1)
        return (own_half + update).astype(jnp.bfloat16)

    embedded_all = lookup_rows(flat_ids, embed_table)

    def tick_whole(tick_pos, state):
        arrived, computed, stored = state
        partner = shifted(arrived, "rep", replicas, 1)
        passed = lax.ppermute(computed, "segment", [(i, i + 1) for i in range(segments - 1)])
        micro_pos = tick_pos - 2 * segment_pos
        active = (micro_pos >= 0) & (micro_pos < micro_count)
        slot_pos = jnp.clip(micro_pos, 0, micro_count - 1)
        embedded = lax.dynamic_slice_in_dim(embedded_all, slot_pos * block_rows, block_rows, 0)
        low = jnp.where(own_first, arrived, partner)
        high = jnp.where(own_first, partner, arrived)
        joined = jnp.concatenate([low, high], axis=1)
        current = jnp.where(is_first, embedded, joined)
        result = apply_segment(current)
        previous = lax.dynamic_slice_in_dim(stored, slot_pos * block_rows, block_rows, 0)
        chosen = jnp.where(active & is_last, result, previous)
        stored = lax.dynamic_update_slice_in_dim(stored, chosen, slot_pos * block_rows, 0)
        return (passed, result, stored)

    initial = (
        jnp.zeros((block_rows, half_width), jnp.bfloat16),
        jnp.zeros((block_rows, half_width), jnp.bfloat16),
        jnp.zeros((total_rows, half_width), jnp.bfloat16),
    )
    final_half = lax.fori_loop(0, tick_count, tick_whole, initial)[2]

    positions = jnp.arange(seq_len, dtype=jnp.int32)
    next_ids = jnp.concatenate([token_ids[:, 1:], token_ids[:, :1]], axis=1)
    live_mask = (positions[None, :] < seq_lengths[:, None] - 1).astype(jnp.float32)
    counts = (seq_lengths - 1).astype(jnp.float32)

    wide_half = final_half.astype(jnp.float32)
    own_squares = jnp.sum(wide_half * wide_half, axis=-1, keepdims=True)
    squares = own_squares + shifted(own_squares, "rep", replicas, 1)
    final_scale = lax.rsqrt(squares / model_width + epsilon)
    gain_half = lax.dynamic_slice_in_dim(final_gain, rep_pos * half_width, half_width, 0)
    head_half = lax.dynamic_slice_in_dim(head_weight, rep_pos * half_width, half_width, 0)
    prior_half = (wide_half * final_scale * gain_half).astype(jnp.bfloat16)
    own_logits = jnp.dot(prior_half, head_half, preferred_element_type=jnp.float32)
    prior_logits = own_logits + shifted(own_logits, "rep", replicas, 1)
    prior_logp = jax.nn.log_softmax(prior_logits, axis=-1)
    token_terms = picked_logprob(prior_logp, next_ids.reshape(-1)).reshape(group_seqs, seq_len)
    prior_group = jnp.sum(token_terms * live_mask, axis=1) / counts
    from_last = prior_group
    for by in range(1, segments):
        moved = shifted(prior_group, "segment", segments, by)
        from_last = jnp.where((segment_pos - by) % segments == segments - 1, moved, from_last)
    prior_group = from_last

    own_seq = (segment_pos * replicas + rep_pos) * per_device
    prior_mine = lax.dynamic_slice_in_dim(prior_group, own_seq, per_device, 0)
    mine_ids = lax.dynamic_slice_in_dim(token_ids, own_seq, per_device, 0).reshape(-1)
    mine_next = lax.dynamic_slice_in_dim(next_ids, own_seq, per_device, 0).reshape(-1)
    mine_live = lax.dynamic_slice_in_dim(live_mask, own_seq, per_device, 0)
    mine_counts = lax.dynamic_slice_in_dim(counts, own_seq, per_device, 0)
    mine_scores = lax.dynamic_slice_in_dim(quant_scores, own_seq, per_device, 0)
    start_wide = lookup_rows(mine_ids, embed_table).astype(jnp.float32)
    unit_rows = (start_wide * rms_scale(start_wide)).astype(jnp.bfloat16)
    latent = jnp.dot(unit_rows, down_full, preferred_element_type=jnp.float32).astype(jnp.bfloat16)
    hidden = start_wide + lax.dot_general(
        latent, up_full, (((1,), (1,)), ((), ())), preferred_element_type=jnp.float32
    )
    inverse = rms_scale(hidden)
    agent_final = (hidden * inverse * final_gain).astype(jnp.bfloat16)
    logprob = jax.nn.log_softmax(
        jnp.dot(agent_final, head_weight, preferred_element_type=jnp.float32), axis=-1
    )
    agent_ll = (
        jnp.sum(picked_logprob(logprob, mine_next).reshape(per_device, seq_len) * mine_live, axis=1)
        / mine_counts
    )
    margin = prior_mine + sigma_weight * mine_scores.astype(jnp.float32) / LEVELS - agent_ll
    row_factor = ((2.0 * margin / mine_counts)[:, None] * mine_live).reshape(-1)
    column = jnp.arange(vocab_size, dtype=jnp.int32)
    onehot_next = (mine_next[:, None] == column[None, :]).astype(jnp.float32)
    logit_grad = (row_factor[:, None] * (jnp.exp(logprob) - onehot_next)).astype(jnp.bfloat16)
    scaled_grad = (
        lax.dot_general(
            logit_grad, head_weight, (((1,), (1,)), ((), ())), preferred_element_type=jnp.float32
        )
        * final_gain
    )
    hidden_grad = (
        inverse * scaled_grad
        - hidden
        * inverse
        * inverse
        * inverse
        * jnp.mean(hidden * scaled_grad, axis=-1, keepdims=True)
    ).astype(jnp.bfloat16)
    core_pos = lax.axis_index("fsdp") % 2
    along_core = lambda v: fsdp_moved(v, lambda g: g ^ 1)

    def core_columns(values, pick):
        blocks = values.reshape(values.shape[0], 4, 4, 2, 2, 2, model_width // 128)
        return lax.dynamic_index_in_dim(blocks, pick, 4, keepdims=False).reshape(values.shape[0], -1)

    rank = latent.shape[1]
    forward_sent = along_core(jnp.concatenate([core_columns(unit_rows, 1 - core_pos), latent], axis=1))
    latent_grad = jnp.dot(hidden_grad, up_full, preferred_element_type=jnp.float32).astype(
        jnp.bfloat16
    )
    backward_sent = along_core(
        jnp.concatenate([core_columns(hidden_grad, 1 - core_pos), latent_grad], axis=1)
    )
    half_rows = model_width // 2
    unit_both = jnp.concatenate([core_columns(unit_rows, core_pos), forward_sent[:, :half_rows]], axis=0)
    latent_both = jnp.concatenate([latent, forward_sent[:, half_rows:]], axis=0)
    hidden_both = jnp.concatenate([core_columns(hidden_grad, core_pos), backward_sent[:, :half_rows]], axis=0)
    latent_grad_both = jnp.concatenate([latent_grad, backward_sent[:, half_rows:]], axis=0)
    up_grad = lax.dot_general(
        hidden_both, latent_both, (((0,), (0,)), ((), ())), preferred_element_type=jnp.float32
    )
    down_grad = lax.dot_general(
        unit_both, latent_grad_both, (((0,), (0,)), ((), ())), preferred_element_type=jnp.float32
    )
    down_share, up_share = gradient_scatter(down_grad, up_grad)
    return (down_share, up_share)


def solution(mesh):
    placed = (
        P("fsdp", None),
        P("fsdp"),
        P("fsdp"),
        P(),
        P("segment", None, "rep"),
        P("segment", None),
        P(),
        P(),
        P("fsdp", None),
        P("fsdp", None),
    )
    return jax.shard_map(
        on_device,
        mesh=mesh,
        in_specs=placed,
        out_specs=(P(("segment", "fsdp", "rep"), None), P(("segment", "fsdp", "rep"), None)),
        check_vma=False,
    )
```

```python
import jax
import jax.numpy as jnp
from jax import lax
from jax.sharding import PartitionSpec as P

LEVELS = 64


epsilon = 1e-05
sigma_weight = 2.0


def rms_scale(values):
    squares = jnp.mean(values * values, axis=-1, keepdims=True)
    return lax.rsqrt(squares + epsilon)


def lookup_rows(row_ids, embed_table):
    vocab_size = embed_table.shape[0]
    column = jnp.arange(vocab_size, dtype=jnp.int32)
    onehot = (row_ids[:, None] == column[None, :]).astype(jnp.bfloat16)
    return jnp.dot(onehot, embed_table, preferred_element_type=jnp.float32).astype(jnp.bfloat16)


def picked_logprob(logprob, targets):
    vocab_size = logprob.shape[-1]
    column = jnp.arange(vocab_size, dtype=jnp.int32)
    return jnp.sum(jnp.where(column[None, :] == targets[:, None], logprob, 0.0), axis=-1)


def shifted(x, axis, size, by):
    return lax.ppermute(x, axis, [(i, (i + by) % size) for i in range(size)])


def fsdp_moved(x, mapping):
    return lax.ppermute(x, "fsdp", [(f, mapping(f)) for f in range(16)])


def ring_scatter(blocks, me, size, move):
    half = blocks.shape[-1] // 2
    ahead = blocks[..., :half]
    behind = blocks[..., half:]
    cur_a = lax.dynamic_index_in_dim(ahead, (me - 1) % size, 0, keepdims=False)
    cur_b = lax.dynamic_index_in_dim(behind, (me + 1) % size, 0, keepdims=False)
    for step in range(size - 1):
        got_a = move(cur_a, 1)
        got_b = move(cur_b, -1)
        cur_a = got_a + lax.dynamic_index_in_dim(ahead, (me - step - 2) % size, 0, keepdims=False)
        cur_b = got_b + lax.dynamic_index_in_dim(behind, (me + step + 2) % size, 0, keepdims=False)
    return jnp.concatenate([cur_a, cur_b], axis=-1)


def pair_scatter(blocks, axis_pos, me, move):
    keep = lax.dynamic_index_in_dim(blocks, me, axis_pos, keepdims=False)
    send = lax.dynamic_index_in_dim(blocks, 1 - me, axis_pos, keepdims=False)
    return keep + move(send)


def gradient_scatter(first, second):
    rows, cols = first.shape
    seg = lax.axis_index("segment")
    f = lax.axis_index("fsdp")
    rep = lax.axis_index("rep")
    y_pos = f // 4
    zh_pos = (f // 2) % 2
    core_pos = f % 2
    along_x = lambda v, by: shifted(v, "segment", 4, by)
    along_y = lambda v, by: fsdp_moved(v, lambda g: ((g // 4 + by) % 4) * 4 + g % 4)
    along_core = lambda v: fsdp_moved(v, lambda g: g ^ 1)
    along_zh = lambda v: fsdp_moved(v, lambda g: g ^ 2)
    along_zl = lambda v: shifted(v, "rep", 2, 1)
    outs = []
    for grad, order in ((first, 0), (second, 1)):
        blocks = grad.reshape(4, 4, 2, 2, rows // 64, cols)
        if order == 0:
            blocks = ring_scatter(blocks, seg, 4, along_x)
            blocks = ring_scatter(blocks, y_pos, 4, along_y)
        else:
            blocks = jnp.swapaxes(blocks, 0, 1)
            blocks = ring_scatter(blocks, y_pos, 4, along_y)
            blocks = ring_scatter(blocks, seg, 4, along_x)
        outs.append(blocks)
    outs = [pair_scatter(b, 1, rep, along_zl) for b in outs]
    outs = [pair_scatter(b, 0, zh_pos, along_zh) for b in outs]
    return outs


def on_device(
    token_ids,
    seq_lengths,
    quant_scores,
    embed_table,
    prior_weight,
    prior_gain,
    final_gain,
    head_weight,
    agent_down,
    agent_up,
):
    segments = lax.axis_size("segment")
    replicas = lax.axis_size("rep")
    segment_pos = lax.axis_index("segment")
    rep_pos = lax.axis_index("rep")
    group_seqs, seq_len = token_ids.shape
    model_width = embed_table.shape[1]
    vocab_size = embed_table.shape[0]
    half_width = prior_weight.shape[2]
    per_device = group_seqs // (segments * replicas)
    micro_count = 8
    total_rows = group_seqs * seq_len
    block_rows = total_rows // micro_count
    tick_count = micro_count + 2 * (segments - 1)
    flat_ids = token_ids.reshape(-1)
    weight_local = prior_weight[0]
    gain_local = prior_gain[0]
    is_first = segment_pos == 0
    is_last = segment_pos == segments - 1
    own_first = rep_pos == 0

    both_full = lax.all_gather(jnp.stack([agent_down, agent_up]), "fsdp", axis=1, tiled=True)
    down_full, up_full = both_full[0], both_full[1]

    def apply_segment(current):
        wide_rows = current.astype(jnp.float32)
        normed = (wide_rows * rms_scale(wide_rows) * gain_local).astype(jnp.bfloat16)
        update = jnp.dot(normed, weight_local, preferred_element_type=jnp.float32)
        own_half = lax.dynamic_slice_in_dim(wide_rows, rep_pos * half_width, half_width, 1)
        return (own_half + update).astype(jnp.bfloat16)

    embedded_all = lookup_rows(flat_ids, embed_table)

    def tick_whole(tick_pos, state):
        arrived, computed, stored = state
        partner = shifted(arrived, "rep", replicas, 1)
        passed = lax.ppermute(computed, "segment", [(i, i + 1) for i in range(segments - 1)])
        micro_pos = tick_pos - 2 * segment_pos
        active = (micro_pos >= 0) & (micro_pos < micro_count)
        slot_pos = jnp.clip(micro_pos, 0, micro_count - 1)
        embedded = lax.dynamic_slice_in_dim(embedded_all, slot_pos * block_rows, block_rows, 0)
        low = jnp.where(own_first, arrived, partner)
        high = jnp.where(own_first, partner, arrived)
        joined = jnp.concatenate([low, high], axis=1)
        current = jnp.where(is_first, embedded, joined)
        result = apply_segment(current)
        previous = lax.dynamic_slice_in_dim(stored, slot_pos * block_rows, block_rows, 0)
        chosen = jnp.where(active & is_last, result, previous)
        stored = lax.dynamic_update_slice_in_dim(stored, chosen, slot_pos * block_rows, 0)
        return (passed, result, stored)

    initial = (
        jnp.zeros((block_rows, half_width), jnp.bfloat16),
        jnp.zeros((block_rows, half_width), jnp.bfloat16),
        jnp.zeros((total_rows, half_width), jnp.bfloat16),
    )
    final_half = lax.fori_loop(0, tick_count, tick_whole, initial)[2]

    positions = jnp.arange(seq_len, dtype=jnp.int32)
    next_ids = jnp.concatenate([token_ids[:, 1:], token_ids[:, :1]], axis=1)
    live_mask = (positions[None, :] < seq_lengths[:, None] - 1).astype(jnp.float32)
    counts = (seq_lengths - 1).astype(jnp.float32)

    wide_half = final_half.astype(jnp.float32)
    own_squares = jnp.sum(wide_half * wide_half, axis=-1, keepdims=True)
    squares = own_squares + shifted(own_squares, "rep", replicas, 1)
    final_scale = lax.rsqrt(squares / model_width + epsilon)
    gain_half = lax.dynamic_slice_in_dim(final_gain, rep_pos * half_width, half_width, 0)
    head_half = lax.dynamic_slice_in_dim(head_weight, rep_pos * half_width, half_width, 0)
    prior_half = (wide_half * final_scale * gain_half).astype(jnp.bfloat16)
    own_logits = jnp.dot(prior_half, head_half, preferred_element_type=jnp.float32)
    prior_logits = own_logits + shifted(own_logits, "rep", replicas, 1)
    prior_logp = jax.nn.log_softmax(prior_logits, axis=-1)
    token_terms = picked_logprob(prior_logp, next_ids.reshape(-1)).reshape(group_seqs, seq_len)
    prior_group = jnp.sum(token_terms * live_mask, axis=1) / counts
    from_last = prior_group
    for by in range(1, segments):
        moved = shifted(prior_group, "segment", segments, by)
        from_last = jnp.where((segment_pos - by) % segments == segments - 1, moved, from_last)
    prior_group = from_last

    own_seq = (segment_pos * replicas + rep_pos) * per_device
    prior_mine = lax.dynamic_slice_in_dim(prior_group, own_seq, per_device, 0)
    mine_ids = lax.dynamic_slice_in_dim(token_ids, own_seq, per_device, 0).reshape(-1)
    mine_next = lax.dynamic_slice_in_dim(next_ids, own_seq, per_device, 0).reshape(-1)
    mine_live = lax.dynamic_slice_in_dim(live_mask, own_seq, per_device, 0)
    mine_counts = lax.dynamic_slice_in_dim(counts, own_seq, per_device, 0)
    mine_scores = lax.dynamic_slice_in_dim(quant_scores, own_seq, per_device, 0)
    start_wide = lookup_rows(mine_ids, embed_table).astype(jnp.float32)
    unit_rows = (start_wide * rms_scale(start_wide)).astype(jnp.bfloat16)
    latent = jnp.dot(unit_rows, down_full, preferred_element_type=jnp.float32).astype(jnp.bfloat16)
    hidden = start_wide + lax.dot_general(
        latent, up_full, (((1,), (1,)), ((), ())), preferred_element_type=jnp.float32
    )
    inverse = rms_scale(hidden)
    agent_final = (hidden * inverse * final_gain).astype(jnp.bfloat16)
    logprob = jax.nn.log_softmax(
        jnp.dot(agent_final, head_weight, preferred_element_type=jnp.float32), axis=-1
    )
    agent_ll = (
        jnp.sum(picked_logprob(logprob, mine_next).reshape(per_device, seq_len) * mine_live, axis=1)
        / mine_counts
    )
    margin = prior_mine + sigma_weight * mine_scores.astype(jnp.float32) / LEVELS - agent_ll
    row_factor = ((2.0 * margin / mine_counts)[:, None] * mine_live).reshape(-1)
    column = jnp.arange(vocab_size, dtype=jnp.int32)
    onehot_next = (mine_next[:, None] == column[None, :]).astype(jnp.float32)
    logit_grad = (row_factor[:, None] * (jnp.exp(logprob) - onehot_next)).astype(jnp.bfloat16)
    scaled_grad = (
        lax.dot_general(
            logit_grad, head_weight, (((1,), (1,)), ((), ())), preferred_element_type=jnp.float32
        )
        * final_gain
    )
    hidden_grad = (
        inverse * scaled_grad
        - hidden
        * inverse
        * inverse
        * inverse
        * jnp.mean(hidden * scaled_grad, axis=-1, keepdims=True)
    ).astype(jnp.bfloat16)
    core_pos = lax.axis_index("fsdp") % 2
    along_core = lambda v: fsdp_moved(v, lambda g: g ^ 1)

    def core_columns(values, pick):
        blocks = values.reshape(values.shape[0], 4, 4, 2, 2, 2, model_width // 128)
        return lax.dynamic_index_in_dim(blocks, pick, 4, keepdims=False).reshape(values.shape[0], -1)

    rank = latent.shape[1]
    forward_sent = along_core(jnp.concatenate([core_columns(unit_rows, 1 - core_pos), latent], axis=1))
    latent_grad = jnp.dot(hidden_grad, up_full, preferred_element_type=jnp.float32).astype(
        jnp.bfloat16
    )
    backward_sent = along_core(
        jnp.concatenate([core_columns(hidden_grad, 1 - core_pos), latent_grad], axis=1)
    )
    half_rows = model_width // 2
    unit_both = jnp.concatenate([core_columns(unit_rows, core_pos), forward_sent[:, :half_rows]], axis=0)
    latent_both = jnp.concatenate([latent, forward_sent[:, half_rows:]], axis=0)
    hidden_both = jnp.concatenate([core_columns(hidden_grad, core_pos), backward_sent[:, :half_rows]], axis=0)
    latent_grad_both = jnp.concatenate([latent_grad, backward_sent[:, half_rows:]], axis=0)
    up_grad = lax.dot_general(
        hidden_both, latent_both, (((0,), (0,)), ((), ())), preferred_element_type=jnp.float32
    )
    down_grad = lax.dot_general(
        unit_both, latent_grad_both, (((0,), (0,)), ((), ())), preferred_element_type=jnp.float32
    )
    down_share, up_share = gradient_scatter(down_grad, up_grad)
    return (down_share, up_share)


def solution(mesh):
    placed = (
        P("fsdp", None),
        P("fsdp"),
        P("fsdp"),
        P(),
        P("segment", None, "rep"),
        P("segment", None),
        P(),
        P(),
        P("fsdp", None),
        P("fsdp", None),
    )
    return jax.shard_map(
        on_device,
        mesh=mesh,
        in_specs=placed,
        out_specs=(P(("segment", "fsdp", "rep"), None), P(("segment", "fsdp", "rep"), None)),
        check_vma=False,
    )
```

```python
import jax
import jax.numpy as jnp
from jax import lax
from jax.sharding import PartitionSpec as P

LEVELS = 64


epsilon = 1e-05
sigma_weight = 2.0


def rms_scale(values):
    squares = jnp.mean(values * values, axis=-1, keepdims=True)
    return lax.rsqrt(squares + epsilon)


def lookup_rows(row_ids, embed_table):
    vocab_size = embed_table.shape[0]
    column = jnp.arange(vocab_size, dtype=jnp.int32)
    onehot = (row_ids[:, None] == column[None, :]).astype(jnp.bfloat16)
    return jnp.dot(onehot, embed_table, preferred_element_type=jnp.float32).astype(jnp.bfloat16)


def picked_logprob(logprob, targets):
    vocab_size = logprob.shape[-1]
    column = jnp.arange(vocab_size, dtype=jnp.int32)
    return jnp.sum(jnp.where(column[None, :] == targets[:, None], logprob, 0.0), axis=-1)


def shifted(x, axis, size, by):
    return lax.ppermute(x, axis, [(i, (i + by) % size) for i in range(size)])


def fsdp_moved(x, mapping):
    return lax.ppermute(x, "fsdp", [(f, mapping(f)) for f in range(16)])


def ring_scatter(blocks, me, size, move):
    half = blocks.shape[-1] // 2
    ahead = blocks[..., :half]
    behind = blocks[..., half:]
    cur_a = lax.dynamic_index_in_dim(ahead, (me - 1) % size, 0, keepdims=False)
    cur_b = lax.dynamic_index_in_dim(behind, (me + 1) % size, 0, keepdims=False)
    for step in range(size - 1):
        got_a = move(cur_a, 1)
        got_b = move(cur_b, -1)
        cur_a = got_a + lax.dynamic_index_in_dim(ahead, (me - step - 2) % size, 0, keepdims=False)
        cur_b = got_b + lax.dynamic_index_in_dim(behind, (me + step + 2) % size, 0, keepdims=False)
    return jnp.concatenate([cur_a, cur_b], axis=-1)


def pair_scatter(blocks, axis_pos, me, move):
    keep = lax.dynamic_index_in_dim(blocks, me, axis_pos, keepdims=False)
    send = lax.dynamic_index_in_dim(blocks, 1 - me, axis_pos, keepdims=False)
    return keep + move(send)


def gradient_scatter(first, second):
    rows, cols = first.shape
    seg = lax.axis_index("segment")
    f = lax.axis_index("fsdp")
    rep = lax.axis_index("rep")
    y_pos = f // 4
    zh_pos = (f // 2) % 2
    along_x = lambda v, by: shifted(v, "segment", 4, by)
    along_y = lambda v, by: fsdp_moved(v, lambda g: ((g // 4 + by) % 4) * 4 + g % 4)
    along_zh = lambda v: fsdp_moved(v, lambda g: g ^ 2)
    along_zl = lambda v: shifted(v, "rep", 2, 1)
    outs = []
    for grad, order in ((first, 0), (second, 1)):
        blocks = grad.reshape(4, 4, 2, 2, rows // 64, cols)
        if order == 0:
            blocks = ring_scatter(blocks, seg, 4, along_x)
            blocks = ring_scatter(blocks, y_pos, 4, along_y)
        else:
            blocks = jnp.swapaxes(blocks, 0, 1)
            blocks = ring_scatter(blocks, y_pos, 4, along_y)
            blocks = ring_scatter(blocks, seg, 4, along_x)
        outs.append(blocks)
    outs = [pair_scatter(b, 1, rep, along_zl) for b in outs]
    outs = [pair_scatter(b, 0, zh_pos, along_zh) for b in outs]
    return outs


def on_device(
    token_ids,
    seq_lengths,
    quant_scores,
    embed_table,
    prior_weight,
    prior_gain,
    final_gain,
    head_weight,
    agent_down,
    agent_up,
):
    segments = lax.axis_size("segment")
    replicas = lax.axis_size("rep")
    segment_pos = lax.axis_index("segment")
    rep_pos = lax.axis_index("rep")
    group_seqs, seq_len = token_ids.shape
    model_width = embed_table.shape[1]
    vocab_size = embed_table.shape[0]
    half_width = prior_weight.shape[2]
    per_device = group_seqs // (segments * replicas)
    micro_count = 8
    total_rows = group_seqs * seq_len
    block_rows = total_rows // micro_count
    tick_count = micro_count + 2 * (segments - 1)
    flat_ids = token_ids.reshape(-1)
    weight_local = prior_weight[0]
    gain_local = prior_gain[0]
    is_first = segment_pos == 0
    is_last = segment_pos == segments - 1
    own_first = rep_pos == 0

    both_full = lax.all_gather(jnp.stack([agent_down, agent_up]), "fsdp", axis=1, tiled=True)
    down_full, up_full = both_full[0], both_full[1]

    def apply_segment(current):
        wide_rows = current.astype(jnp.float32)
        normed = (wide_rows * rms_scale(wide_rows) * gain_local).astype(jnp.bfloat16)
        update = jnp.dot(normed, weight_local, preferred_element_type=jnp.float32)
        own_half = lax.dynamic_slice_in_dim(wide_rows, rep_pos * half_width, half_width, 1)
        return (own_half + update).astype(jnp.bfloat16)

    embedded_all = lookup_rows(flat_ids, embed_table)

    def tick_whole(tick_pos, state):
        arrived, computed, stored = state
        partner = shifted(arrived, "rep", replicas, 1)
        passed = lax.ppermute(computed, "segment", [(i, i + 1) for i in range(segments - 1)])
        micro_pos = tick_pos - 2 * segment_pos
        active = (micro_pos >= 0) & (micro_pos < micro_count)
        slot_pos = jnp.clip(micro_pos, 0, micro_count - 1)
        embedded = lax.dynamic_slice_in_dim(embedded_all, slot_pos * block_rows, block_rows, 0)
        low = jnp.where(own_first, arrived, partner)
        high = jnp.where(own_first, partner, arrived)
        joined = jnp.concatenate([low, high], axis=1)
        current = jnp.where(is_first, embedded, joined)
        result = apply_segment(current)
        previous = lax.dynamic_slice_in_dim(stored, slot_pos * block_rows, block_rows, 0)
        chosen = jnp.where(active & is_last, result, previous)
        stored = lax.dynamic_update_slice_in_dim(stored, chosen, slot_pos * block_rows, 0)
        return (passed, result, stored)

    initial = (
        jnp.zeros((block_rows, half_width), jnp.bfloat16),
        jnp.zeros((block_rows, half_width), jnp.bfloat16),
        jnp.zeros((total_rows, half_width), jnp.bfloat16),
    )
    final_half = lax.fori_loop(0, tick_count, tick_whole, initial)[2]

    positions = jnp.arange(seq_len, dtype=jnp.int32)
    next_ids = jnp.concatenate([token_ids[:, 1:], token_ids[:, :1]], axis=1)
    live_mask = (positions[None, :] < seq_lengths[:, None] - 1).astype(jnp.float32)
    counts = (seq_lengths - 1).astype(jnp.float32)

    wide_half = final_half.astype(jnp.float32)
    own_squares = jnp.sum(wide_half * wide_half, axis=-1, keepdims=True)
    squares = own_squares + shifted(own_squares, "rep", replicas, 1)
    final_scale = lax.rsqrt(squares / model_width + epsilon)
    gain_half = lax.dynamic_slice_in_dim(final_gain, rep_pos * half_width, half_width, 0)
    head_half = lax.dynamic_slice_in_dim(head_weight, rep_pos * half_width, half_width, 0)
    prior_half = (wide_half * final_scale * gain_half).astype(jnp.bfloat16)
    own_logits = jnp.dot(prior_half, head_half, preferred_element_type=jnp.float32)
    other_logits = shifted(own_logits, "rep", replicas, 1)
    prior_logits = own_logits + other_logits
    prior_logp = jax.nn.log_softmax(prior_logits, axis=-1)
    token_terms = picked_logprob(prior_logp, next_ids.reshape(-1)).reshape(group_seqs, seq_len)
    prior_group = jnp.sum(token_terms * live_mask, axis=1) / counts
    from_last = prior_group
    for by in range(1, segments):
        moved = shifted(prior_group, "segment", segments, by)
        from_last = jnp.where((segment_pos - by) % segments == segments - 1, moved, from_last)
    prior_group = from_last

    own_seq = (segment_pos * replicas + rep_pos) * per_device
    prior_mine = lax.dynamic_slice_in_dim(prior_group, own_seq, per_device, 0)
    mine_ids = lax.dynamic_slice_in_dim(token_ids, own_seq, per_device, 0).reshape(-1)
    mine_next = lax.dynamic_slice_in_dim(next_ids, own_seq, per_device, 0).reshape(-1)
    mine_live = lax.dynamic_slice_in_dim(live_mask, own_seq, per_device, 0)
    mine_counts = lax.dynamic_slice_in_dim(counts, own_seq, per_device, 0)
    mine_scores = lax.dynamic_slice_in_dim(quant_scores, own_seq, per_device, 0)
    start_wide = lookup_rows(mine_ids, embed_table).astype(jnp.float32)
    unit_rows = (start_wide * rms_scale(start_wide)).astype(jnp.bfloat16)
    latent = jnp.dot(unit_rows, down_full, preferred_element_type=jnp.float32).astype(jnp.bfloat16)
    hidden = start_wide + lax.dot_general(latent, up_full, (((1,), (1,)), ((), ())), preferred_element_type=jnp.float32)
    inverse = rms_scale(hidden)
    agent_final = (hidden * inverse * final_gain).astype(jnp.bfloat16)
    logprob = jax.nn.log_softmax(
        jnp.dot(agent_final, head_weight, preferred_element_type=jnp.float32), axis=-1
    )
    agent_ll = (
        jnp.sum(picked_logprob(logprob, mine_next).reshape(per_device, seq_len) * mine_live, axis=1)
        / mine_counts
    )
    margin = prior_mine + sigma_weight * mine_scores.astype(jnp.float32) / LEVELS - agent_ll
    row_factor = ((2.0 * margin / mine_counts)[:, None] * mine_live).reshape(-1)
    column = jnp.arange(vocab_size, dtype=jnp.int32)
    onehot_next = (mine_next[:, None] == column[None, :]).astype(jnp.float32)
    logit_grad = (row_factor[:, None] * (jnp.exp(logprob) - onehot_next)).astype(jnp.bfloat16)
    scaled_grad = (
        lax.dot_general(
            logit_grad, head_weight, (((1,), (1,)), ((), ())), preferred_element_type=jnp.float32
        )
        * final_gain
    )
    hidden_grad = (
        inverse * scaled_grad
        - hidden
        * inverse
        * inverse
        * inverse
        * jnp.mean(hidden * scaled_grad, axis=-1, keepdims=True)
    ).astype(jnp.bfloat16)
    core_pos = lax.axis_index("fsdp") % 2
    along_core = lambda v: fsdp_moved(v, lambda g: g ^ 1)

    def core_columns(values, pick):
        blocks = values.reshape(values.shape[0], 4, 4, 2, 2, 2, model_width // 128)
        return lax.dynamic_index_in_dim(blocks, pick, 4, keepdims=False).reshape(values.shape[0], -1)

    forward_given = jnp.concatenate([core_columns(unit_rows, 1 - core_pos), latent], axis=1)
    forward_sent = along_core(forward_given)
    latent_grad = jnp.dot(hidden_grad, up_full, preferred_element_type=jnp.float32).astype(
        jnp.bfloat16
    )
    backward_sent = along_core(
        jnp.concatenate([core_columns(hidden_grad, 1 - core_pos), latent_grad], axis=1)
    )
    half_rows = model_width // 2
    unit_both = jnp.concatenate([core_columns(unit_rows, core_pos), forward_sent[:, :half_rows]], axis=0)
    latent_both = jnp.concatenate([latent, forward_sent[:, half_rows:]], axis=0)
    hidden_both = jnp.concatenate([core_columns(hidden_grad, core_pos), backward_sent[:, :half_rows]], axis=0)
    latent_grad_both = jnp.concatenate([latent_grad, backward_sent[:, half_rows:]], axis=0)
    up_grad = lax.dot_general(
        hidden_both, latent_both, (((0,), (0,)), ((), ())), preferred_element_type=jnp.float32
    )
    down_grad = lax.dot_general(
        unit_both, latent_grad_both, (((0,), (0,)), ((), ())), preferred_element_type=jnp.float32
    )
    down_share, up_share = gradient_scatter(down_grad, up_grad)
    return (down_share, up_share)


def solution(mesh):
    placed = (
        P("fsdp", None),
        P("fsdp"),
        P("fsdp"),
        P(),
        P("segment", None, "rep"),
        P("segment", None),
        P(),
        P(),
        P("fsdp", None),
        P("fsdp", None),
    )

    return jax.shard_map(
        on_device,
        mesh=mesh,
        in_specs=placed,
        out_specs=(P(("segment", "fsdp", "rep"), None), P(("segment", "fsdp", "rep"), None)),
        check_vma=False,
    )
```
